32 devices in a mesh: cell: 8 (over y, x, core), gene: 4 (over z).
Axes of the slice: x: 2, y: 2, z: 4, core: 2. Of those that a mesh axis runs over, the one named last changes fastest.
Arguments:
- expression: float32 [12288, 32768], P('cell', 'gene'), may hold values from -16 to 18, as said below
- tile_mask: int32 [48, 128], P('cell', 'gene'), may hold values from 0 to 1, as said below
- start: float32 [32768, 32], P('gene'), may hold values from -6 to 6
Outputs:
- alphas: float32 [2, 32, 32], replicated
- betas: float32 [2, 32, 32], replicated
- next_block: float32 [32768, 32], P('gene')
The draws below stay inside these ranges and needn't reach their ends.
Inputs may be any that keep to these rules, and one draw needn't show every extreme that they name: expression: positive mean per gene with gene and cell scales and independent noise. `tile_mask`: each row of tiles belongs to one of 8 cell types and each column of tiles to one of 8 gene modules; a tile is 1 where its type expresses its module.
All inputs are finite; a program needn't handle non-finite values.
Results may differ from the reference program's by a relative error of at most 0.0024.
Values sent between devices are 32-bit elements; how exact they have to be, the bound alone decides.
No kernel may reach another device: no remote copies, remote signals or barrier semaphores. Data moves between devices by JAX's collectives and lax.ppermute only.
A program may use at most 256 MiB of HBM per device.

```python
import jax
import jax.numpy as jnp
from jax import lax

CELL_DEV = 1536
GENES = 32768
TILE = 256
BLOCK = 32
STEPS = 2
CELLS = 12288
N_CELL = 8


def draw_expression(key, part):
    keys = jax.random.split(key, 3)
    gene_scale = jnp.exp(jax.random.uniform(keys[0], (1, GENES), jnp.float32, -0.7, 0.7))
    cell_scale = jnp.exp(jax.random.uniform(keys[1], (CELLS, 1), jnp.float32, -0.7, 0.7))
    noise = jnp.clip(jax.random.normal(keys[2], (CELLS, GENES), jnp.float32), -4.0, 4.0)
    return gene_scale * (0.6 + cell_scale * noise)


def draw_tile_mask(key, part):
    keys = jax.random.split(key, 3)
    types = jax.random.randint(keys[0], (CELLS // TILE,), 0, 8)
    modules = jax.random.randint(keys[1], (GENES // TILE,), 0, 8)
    table = jnp.maximum(jax.random.randint(keys[2], (8, 8), 0, 2), jnp.eye(8, dtype=jnp.int32))
    return jnp.take(jnp.take(table, types, axis=0), modules, axis=1).astype(jnp.int32)


def steps_of(own_key, shape, cuts, low, high):
    gain = 1.0
    for dim, parts in cuts:
        draws = jax.random.uniform(jax.random.fold_in(jax.random.fold_in(own_key, 6), dim), (parts,), jnp.float32, low / len(cuts), high / len(cuts))
        gain = gain * jnp.repeat(jnp.exp(draws), shape[dim] // parts).reshape((-1,) + (1,) * (len(shape) - 1 - dim))
    return gain


def gaussian(rng, dims, scale, limit, cuts=(), held_as=jnp.bfloat16):
    drawn = scale * jax.random.normal(rng, dims, jnp.float32)
    if cuts:
        drawn = drawn * steps_of(rng, dims, cuts, -0.22, 0.18)
    return jnp.clip(drawn, -limit, limit).astype(held_as)


def setup_inputs(seed: int = 0) -> dict:
    arg_keys = jax.random.split(jax.random.key(seed), 4)
    return {
        "expression": draw_expression(jax.random.fold_in(arg_keys[3], 71), 0),
        "tile_mask": draw_tile_mask(jax.random.fold_in(arg_keys[3], 71), 0),
        "start": gaussian(arg_keys[2], (GENES, BLOCK), 1.0, 6.0, ((0, 4),), jnp.float32),
    }


highest = lax.Precision.HIGHEST

def transposed_dot(left, right):
    return lax.dot_general(left.astype(jnp.float32), right.astype(jnp.float32), (((0,), (0,)), ((), ())), precision=highest, preferred_element_type=jnp.float32)

def product(left, right):
    return jnp.dot(left.astype(jnp.float32), right.astype(jnp.float32), precision=highest, preferred_element_type=jnp.float32)

def finish(resid, gram):
    lower = jnp.linalg.cholesky(gram)
    fresh = lax.linalg.triangular_solve(lower, resid, left_side=False, lower=True, transpose_a=True)
    return (fresh, jnp.transpose(lower))

def reference(expression, tile_mask, start):
    blocks = expression.reshape(N_CELL, CELL_DEV, GENES)
    masks = tile_mask.reshape(N_CELL, CELL_DEV // TILE, GENES // TILE)

    def masked_block(values, occupancy):
        tiles = values.reshape(CELL_DEV // TILE, TILE, GENES // TILE, TILE)
        return (tiles * occupancy.astype(jnp.float32)[:, None, :, None]).reshape(CELL_DEV, GENES)

    def add_means(total, pair):
        return (total + jnp.sum(masked_block(pair[0], pair[1]), axis=0), None)
    col_total = lax.scan(add_means, jnp.zeros((GENES,), jnp.float32), (blocks, masks))[0]
    means = col_total / CELLS

    def apply_gram(current):

        def side(pair):
            return product(masked_block(pair[0], pair[1]), current) - product(means[None, :], current)
        cell_side = lax.map(side, (blocks, masks))

        def add_image(total, triple):
            return (total + transposed_dot(masked_block(triple[0], triple[1]), triple[2]), None)
        summed = lax.scan(add_image, jnp.zeros((GENES, BLOCK), jnp.float32), (blocks, masks, cell_side))[0]
        return summed / CELLS
    current = finish(start, transposed_dot(start, start))[0]
    older = None
    alpha_list = []
    beta_list = []
    for step in range(STEPS):
        image = apply_gram(current)
        alpha = transposed_dot(current, image)
        resid = image - product(current, alpha)
        if older is not None:
            prior = transposed_dot(older, image)
            resid = resid - product(older, prior)
        fresh, beta = finish(resid, transposed_dot(resid, resid))
        alpha_list.append(alpha)
        beta_list.append(beta)
        older = current
        current = fresh
    return (jnp.stack(alpha_list), jnp.stack(beta_list), current * GENES ** 0.5)
```

```python
import math

import jax
import jax.numpy as jnp
from jax import lax
from jax.experimental import pallas as pl
from jax.experimental.pallas import tpu as pltpu
from jax.sharding import PartitionSpec as P

TILE = 256
STEPS = 2
BF = jnp.bfloat16
F32 = jnp.float32


def split(x):
    p1 = x.astype(BF)
    r1 = x - p1.astype(F32)
    p2 = r1.astype(BF)
    p3 = (r1 - p2.astype(F32)).astype(BF)
    return p1, p2, p3


def split_outside(x):
    pieces = []
    rest = x
    for _ in range(2):
        t = rest * 65537.0
        head = t - (t - rest)
        pieces.append(head.astype(BF))
        rest = rest - head
    pieces.append(rest.astype(BF))
    return pieces


def stacks(p, axis):
    return (jnp.concatenate(p, axis=axis), jnp.concatenate(p[:2], axis=axis), p[0])


def butterfly_sum(x, axis):
    n = lax.axis_size(axis)
    if n & (n - 1):
        return lax.psum(x, axis)
    s = 1
    while s < n:
        x = x + lax.ppermute(x, axis, [(i, i ^ s) for i in range(n)])
        s *= 2
    return x


def halving_sum(x, axis, dim):
    n = lax.axis_size(axis)
    if n & (n - 1) or x.shape[dim] % n:
        return lax.psum(x, axis)
    me = lax.axis_index(axis)
    s = 1
    bits = []
    while s < n:
        half = x.shape[dim] // 2
        bit = (me // s) % 2
        keep = lax.dynamic_slice_in_dim(x, bit * half, half, axis=dim)
        send = lax.dynamic_slice_in_dim(x, (1 - bit) * half, half, axis=dim)
        x = keep + lax.ppermute(send, axis, [(i, i ^ s) for i in range(n)])
        bits.append((s, bit))
        s *= 2
    for s, bit in reversed(bits):
        other = lax.ppermute(x, axis, [(i, i ^ s) for i in range(n)])
        lo_first = jnp.concatenate([x, other], axis=dim)
        hi_first = jnp.concatenate([other, x], axis=dim)
        x = jnp.where(bit == 0, lo_first, hi_first)
    return x


def _masked_rows(x_ref, m_ref):
    return x_ref[...] * m_ref[0]


def forward_kernel(x_ref, m_ref, s3_ref, s2_ref, s1_ref, y_ref, *col):
    j = pl.program_id(1)
    x = _masked_rows(x_ref, m_ref)
    x1, x2, x3 = split(x)
    k = s1_ref.shape[1]
    a = jnp.dot(x1, s3_ref[...], preferred_element_type=F32)
    c = jnp.dot(x2, s2_ref[...], preferred_element_type=F32)
    d = jnp.dot(x3, s1_ref[...], preferred_element_type=F32)
    part = ((a[:, 2 * k:] + c[:, k:] + d) + (a[:, k:2 * k] + c[:, :k])) + a[:, :k]

    @pl.when(j == 0)
    def _():
        y_ref[...] = part

    @pl.when(j > 0)
    def _():
        y_ref[...] += part

    if col:
        (c_ref,) = col
        i = pl.program_id(0)
        tw = x_ref.shape[1]
        s = jnp.sum(x, axis=0, keepdims=True)
        sl = pl.ds(pl.multiple_of(j * tw, tw), tw)

        @pl.when(i == 0)
        def _():
            c_ref[:, sl] = s

        @pl.when(i > 0)
        def _():
            c_ref[:, sl] += s


def backward_kernel(x_ref, m_ref, s3_ref, s2_ref, s1_ref, o_ref):
    i = pl.program_id(1)
    x = _masked_rows(x_ref, m_ref)
    x1, x2, x3 = split(x)
    k = s1_ref.shape[0]
    a = jnp.dot(s3_ref[...], x1, preferred_element_type=F32)
    c = jnp.dot(s2_ref[...], x2, preferred_element_type=F32)
    d = jnp.dot(s1_ref[...], x3, preferred_element_type=F32)
    part = ((a[2 * k:] + c[k:] + d) + (a[k:2 * k] + c[:k])) + a[:k]

    @pl.when(i == 0)
    def _():
        o_ref[...] = part

    @pl.when(i > 0)
    def _():
        o_ref[...] += part


def blocks(rows, width):
    tr = TILE
    tw = min(width, 4096)
    return tr, tw


def forward(expression, mexp, b, with_colsum):
    rows, width = expression.shape
    k = b.shape[1]
    tr, tw = blocks(rows, width)
    s3, s2, s1 = stacks(split_outside(b), 1)
    grid = (rows // tr, width // tw)
    in_specs = [
        pl.BlockSpec((tr, tw), lambda i, j: (i, j)),
        pl.BlockSpec((1, 1, tw), lambda i, j: (i, 0, j)),
        pl.BlockSpec((tw, 3 * k), lambda i, j: (j, 0)),
        pl.BlockSpec((tw, 2 * k), lambda i, j: (j, 0)),
        pl.BlockSpec((tw, k), lambda i, j: (j, 0)),
    ]
    out_specs = [pl.BlockSpec((tr, k), lambda i, j: (i, 0))]
    out_shape = [jax.ShapeDtypeStruct((rows, k), F32)]
    if with_colsum:
        out_specs.append(pl.BlockSpec((1, width), lambda i, j: (0, 0)))
        out_shape.append(jax.ShapeDtypeStruct((1, width), F32))
    res = pl.pallas_call(
        forward_kernel,
        grid=grid,
        in_specs=in_specs,
        out_specs=out_specs,
        out_shape=out_shape,
        compiler_params=pltpu.CompilerParams(dimension_semantics=("arbitrary", "arbitrary")),
    )(expression, mexp, s3, s2, s1)
    return res


def backward(expression, mexp, y):
    rows, width = expression.shape
    k = y.shape[1]
    tr, tw = blocks(rows, width)
    yt = jnp.transpose(y)
    s3, s2, s1 = stacks(split_outside(yt), 0)
    grid = (width // tw, rows // tr)
    return pl.pallas_call(
        backward_kernel,
        grid=grid,
        in_specs=[
            pl.BlockSpec((tr, tw), lambda j, i: (i, j)),
            pl.BlockSpec((1, 1, tw), lambda j, i: (i, 0, j)),
            pl.BlockSpec((3 * k, tr), lambda j, i: (0, i)),
            pl.BlockSpec((2 * k, tr), lambda j, i: (0, i)),
            pl.BlockSpec((k, tr), lambda j, i: (0, i)),
        ],
        out_specs=pl.BlockSpec((k, tw), lambda j, i: (0, j)),
        out_shape=jax.ShapeDtypeStruct((k, width), F32),
        compiler_params=pltpu.CompilerParams(dimension_semantics=("arbitrary", "arbitrary")),
    )(expression, mexp, s3, s2, s1)


def gram(a):
    return lax.dot_general(a, a, (((0,), (0,)), ((), ())), precision=lax.Precision.HIGHEST,
                           preferred_element_type=F32)


def tdot(a, b):
    return lax.dot_general(a, b, (((0,), (0,)), ((), ())), precision=lax.Precision.HIGHEST,
                           preferred_element_type=F32)


def mm(a, b):
    return jnp.dot(a, b, precision=lax.Precision.HIGHEST, preferred_element_type=F32)


def right_solve(lower, x):
    return lax.linalg.triangular_solve(lower, x, left_side=False, lower=True, transpose_a=True)


def per_device(expression, tile_mask, start):
    cell_count = lax.axis_size("cell")
    gene_count = lax.axis_size("gene")
    rows, width = expression.shape
    cells = rows * cell_count
    mexp = jnp.repeat(tile_mask.astype(F32), TILE, axis=1)[:, None, :]

    gram0 = butterfly_sum(gram(start), "gene")
    lower0 = jnp.linalg.cholesky(gram0)
    current = right_solve(lower0, start)

    y_start, colsum = forward(expression, mexp, start, True)
    means = butterfly_sum(colsum[0], "cell") / cells
    y = right_solve(lower0, halving_sum(y_start, "gene", 0))

    older = None
    alpha_list = []
    beta_list = []
    for step in range(STEPS):
        if step > 0:
            y = halving_sum(forward(expression, mexp, current, False)[0], "gene", 0)
        mean_side = butterfly_sum(jnp.dot(means, current, precision=lax.Precision.HIGHEST), "gene")
        raw = halving_sum(backward(expression, mexp, y), "cell", 1)
        image = jnp.transpose(raw) / cells - means[:, None] * mean_side[None, :]
        proj = [tdot(current, image)]
        if older is not None:
            proj.append(tdot(older, image))
        summed = butterfly_sum(jnp.stack(proj), "gene")
        resid = image - mm(current, summed[0])
        if older is not None:
            resid = resid - mm(older, summed[1])
        g = butterfly_sum(gram(resid), "gene")
        lower = jnp.linalg.cholesky(g)
        fresh = right_solve(lower, resid)
        alpha_list.append(summed[0])
        beta_list.append(jnp.transpose(lower))
        older = current
        current = fresh
    next_block = current * math.sqrt(width * gene_count)
    return (jnp.stack(alpha_list), jnp.stack(beta_list), next_block)


def solution(mesh):
    in_specs = (P("cell", "gene"), P("cell", "gene"), P("gene", None))
    out_specs = (P(), P(), P("gene", None))
    return jax.shard_map(
        per_device, mesh=mesh, in_specs=in_specs, out_specs=out_specs, check_vma=False
    )
```

```python
import math

import jax
import jax.numpy as jnp
from jax import lax
from jax.experimental import pallas as pl
from jax.experimental.pallas import tpu as pltpu
from jax.sharding import PartitionSpec as P

TILE = 256
STEPS = 2
BF = jnp.bfloat16
F32 = jnp.float32


def split(x):
    p1 = x.astype(BF)
    r1 = x - p1.astype(F32)
    p2 = r1.astype(BF)
    p3 = (r1 - p2.astype(F32)).astype(BF)
    return p1, p2, p3


def split_outside(x):
    pieces = []
    rest = x
    for _ in range(2):
        t = rest * 65537.0
        head = t - (t - rest)
        pieces.append(head.astype(BF))
        rest = rest - head
    pieces.append(rest.astype(BF))
    return pieces


def stacks(p, axis):
    return (jnp.concatenate(p, axis=axis), jnp.concatenate(p[:2], axis=axis), p[0])


def butterfly_sum(x, axis):
    n = lax.axis_size(axis)
    if n & (n - 1):
        return lax.psum(x, axis)
    s = 1
    while s < n:
        x = x + lax.ppermute(x, axis, [(i, i ^ s) for i in range(n)])
        s *= 2
    return x


def halving_sum(x, axis, dim):
    n = lax.axis_size(axis)
    if n & (n - 1) or x.shape[dim] % n:
        return lax.psum(x, axis)
    me = lax.axis_index(axis)
    s = 1
    bits = []
    while s < n:
        half = x.shape[dim] // 2
        bit = (me // s) % 2
        keep = lax.dynamic_slice_in_dim(x, bit * half, half, axis=dim)
        send = lax.dynamic_slice_in_dim(x, (1 - bit) * half, half, axis=dim)
        x = keep + lax.ppermute(send, axis, [(i, i ^ s) for i in range(n)])
        bits.append((s, bit))
        s *= 2
    for s, bit in reversed(bits):
        other = lax.ppermute(x, axis, [(i, i ^ s) for i in range(n)])
        lo_first = jnp.concatenate([x, other], axis=dim)
        hi_first = jnp.concatenate([other, x], axis=dim)
        x = jnp.where(bit == 0, lo_first, hi_first)
    return x


def _nt(a, b):
    return lax.dot_general(a, b, (((1,), (1,)), ((), ())), preferred_element_type=F32)


def forward_kernel(mask_ref, x_ref, s3_ref, s2_ref, s1_ref, y_ref, *col):
    i = pl.program_id(0)
    j = pl.program_id(1)
    k = s1_ref.shape[0]
    tiles = x_ref.shape[1] // TILE

    @pl.when(j == 0)
    def _():
        y_ref[...] = jnp.zeros_like(y_ref)

    if col:
        (c_ref,) = col

        @pl.when((i == 0) & (j == 0))
        def _():
            c_ref[...] = jnp.zeros_like(c_ref)

    def body(t, carry):
        m = mask_ref[i, j * tiles + t]
        lanes = pl.ds(pl.multiple_of(t * TILE, TILE), TILE)

        @pl.when(m != 0)
        def _():
            x = x_ref[:, lanes] * m.astype(F32)
            x1, x2, x3 = split(x)
            a = _nt(x1, s3_ref[:, lanes])
            c = _nt(x2, s2_ref[:, lanes])
            d = _nt(x3, s1_ref[:, lanes])
            y_ref[...] += ((a[:, 2 * k:] + c[:, k:] + d) + (a[:, k:2 * k] + c[:, :k])) + a[:, :k]
            if col:
                at = pl.ds(pl.multiple_of((j * tiles + t) * TILE, TILE), TILE)
                c_ref[:, at] += jnp.sum(x, axis=0, keepdims=True)

        return carry

    lax.fori_loop(0, tiles, body, 0)


def backward_kernel(mask_ref, x_ref, s3_ref, s2_ref, s1_ref, o_ref):
    i = pl.program_id(1)
    j = pl.program_id(0)
    k = s1_ref.shape[0]
    tiles = x_ref.shape[1] // TILE

    @pl.when(i == 0)
    def _():
        o_ref[...] = jnp.zeros_like(o_ref)

    def body(t, carry):
        m = mask_ref[i, j * tiles + t]
        lanes = pl.ds(pl.multiple_of(t * TILE, TILE), TILE)

        @pl.when(m != 0)
        def _():
            x = x_ref[:, lanes] * m.astype(F32)
            x1, x2, x3 = split(x)
            a = jnp.dot(s3_ref[...], x1, preferred_element_type=F32)
            c = jnp.dot(s2_ref[...], x2, preferred_element_type=F32)
            d = jnp.dot(s1_ref[...], x3, preferred_element_type=F32)
            o_ref[:, lanes] += ((a[2 * k:] + c[k:] + d) + (a[k:2 * k] + c[:k])) + a[:k]

        return carry

    lax.fori_loop(0, tiles, body, 0)


def blocks(rows, width):
    tr = TILE
    tw = min(width, 4096)
    return tr, tw


def forward(expression, mask, bt, with_colsum):
    rows, width = expression.shape
    k = bt.shape[0]
    tr, tw = blocks(rows, width)
    s3, s2, s1 = stacks(split_outside(bt), 0)
    in_specs = [
        pl.BlockSpec((tr, tw), lambda i, j, m: (i, j)),
        pl.BlockSpec((3 * k, tw), lambda i, j, m: (0, j)),
        pl.BlockSpec((2 * k, tw), lambda i, j, m: (0, j)),
        pl.BlockSpec((k, tw), lambda i, j, m: (0, j)),
    ]
    out_specs = [pl.BlockSpec((tr, k), lambda i, j, m: (i, 0))]
    out_shape = [jax.ShapeDtypeStruct((rows, k), F32)]
    if with_colsum:
        out_specs.append(pl.BlockSpec((1, width), lambda i, j, m: (0, 0)))
        out_shape.append(jax.ShapeDtypeStruct((1, width), F32))
    return pl.pallas_call(
        forward_kernel,
        grid_spec=pltpu.PrefetchScalarGridSpec(
            num_scalar_prefetch=1, grid=(rows // tr, width // tw),
            in_specs=in_specs, out_specs=out_specs),
        out_shape=out_shape,
        compiler_params=pltpu.CompilerParams(dimension_semantics=("arbitrary", "arbitrary")),
    )(mask, expression, s3, s2, s1)


def backward(expression, mask, y):
    rows, width = expression.shape
    k = y.shape[1]
    tr, tw = blocks(rows, width)
    s3, s2, s1 = stacks(split_outside(jnp.transpose(y)), 0)
    return pl.pallas_call(
        backward_kernel,
        grid_spec=pltpu.PrefetchScalarGridSpec(
            num_scalar_prefetch=1, grid=(width // tw, rows // tr),
            in_specs=[
                pl.BlockSpec((tr, tw), lambda j, i, m: (i, j)),
                pl.BlockSpec((3 * k, tr), lambda j, i, m: (0, i)),
                pl.BlockSpec((2 * k, tr), lambda j, i, m: (0, i)),
                pl.BlockSpec((k, tr), lambda j, i, m: (0, i)),
            ],
            out_specs=pl.BlockSpec((k, tw), lambda j, i, m: (0, j))),
        out_shape=jax.ShapeDtypeStruct((k, width), F32),
        compiler_params=pltpu.CompilerParams(dimension_semantics=("arbitrary", "arbitrary")),
    )(mask, expression, s3, s2, s1)


HI = lax.Precision.HIGHEST


def row_gram(a, b):
    return lax.dot_general(a, b, (((1,), (1,)), ((), ())), precision=HI, preferred_element_type=F32)


def left_solve(lower, x):
    return lax.linalg.triangular_solve(lower, x, left_side=True, lower=True)


def right_solve(lower, x):
    return lax.linalg.triangular_solve(lower, x, left_side=False, lower=True, transpose_a=True)


def per_device(expression, tile_mask, start):
    cell_count = lax.axis_size("cell")
    gene_count = lax.axis_size("gene")
    rows, width = expression.shape
    cells = rows * cell_count

    start_t = jnp.transpose(start)
    gram0 = butterfly_sum(row_gram(start_t, start_t), "gene")
    lower0 = jnp.linalg.cholesky(gram0)
    current = left_solve(lower0, start_t)

    y_start, colsum = forward(expression, tile_mask, start_t, True)
    means = butterfly_sum(colsum[0], "cell") / cells
    y = right_solve(lower0, butterfly_sum(y_start, "gene"))

    older = None
    alpha_list = []
    beta_list = []
    for step in range(STEPS):
        if step > 0:
            y = butterfly_sum(forward(expression, tile_mask, current, False)[0], "gene")
        mean_side = butterfly_sum(jnp.dot(current, means, precision=HI), "gene")
        raw = halving_sum(backward(expression, tile_mask, y), "cell", 1)
        image = raw / cells - mean_side[:, None] * means[None, :]
        proj = [row_gram(current, image)]
        if older is not None:
            proj.append(row_gram(older, image))
        summed = butterfly_sum(jnp.stack(proj), "gene")
        resid = image - jnp.dot(jnp.transpose(summed[0]), current, precision=HI)
        if older is not None:
            resid = resid - jnp.dot(jnp.transpose(summed[1]), older, precision=HI)
        g = butterfly_sum(row_gram(resid, resid), "gene")
        lower = jnp.linalg.cholesky(g)
        fresh = left_solve(lower, resid)
        alpha_list.append(summed[0])
        beta_list.append(jnp.transpose(lower))
        older = current
        current = fresh
    next_block = jnp.transpose(current) * math.sqrt(width * gene_count)
    return (jnp.stack(alpha_list), jnp.stack(beta_list), next_block)


def solution(mesh):
    in_specs = (P("cell", "gene"), P("cell", "gene"), P("gene", None))
    out_specs = (P(), P(), P("gene", None))
    return jax.shard_map(
        per_device, mesh=mesh, in_specs=in_specs, out_specs=out_specs, check_vma=False
    )
```

```python
import math

import jax
import jax.numpy as jnp
from jax import lax
from jax.experimental import pallas as pl
from jax.experimental.pallas import tpu as pltpu
from jax.sharding import PartitionSpec as P

TILE = 256
STEPS = 2
BF = jnp.bfloat16
F32 = jnp.float32


def split(x):
    p1 = x.astype(BF)
    r1 = x - p1.astype(F32)
    p2 = r1.astype(BF)
    p3 = (r1 - p2.astype(F32)).astype(BF)
    return p1, p2, p3


def split_outside(x):
    pieces = []
    rest = x
    for _ in range(2):
        t = rest * 65537.0
        head = t - (t - rest)
        pieces.append(head.astype(BF))
        rest = rest - head
    pieces.append(rest.astype(BF))
    return pieces


def stacks(p, axis):
    return (jnp.concatenate(p, axis=axis), jnp.concatenate(p[:2], axis=axis), p[0])


def butterfly_sum(x, axis):
    n = lax.axis_size(axis)
    if n & (n - 1):
        return lax.psum(x, axis)
    s = 1
    while s < n:
        x = x + lax.ppermute(x, axis, [(i, i ^ s) for i in range(n)])
        s *= 2
    return x


def halving_sum(x, axis, dim):
    n = lax.axis_size(axis)
    if n & (n - 1) or x.shape[dim] % n:
        return lax.psum(x, axis)
    me = lax.axis_index(axis)
    s = 1
    bits = []
    while s < n:
        half = x.shape[dim] // 2
        bit = (me // s) % 2
        keep = lax.dynamic_slice_in_dim(x, bit * half, half, axis=dim)
        send = lax.dynamic_slice_in_dim(x, (1 - bit) * half, half, axis=dim)
        x = keep + lax.ppermute(send, axis, [(i, i ^ s) for i in range(n)])
        bits.append((s, bit))
        s *= 2
    for s, bit in reversed(bits):
        other = lax.ppermute(x, axis, [(i, i ^ s) for i in range(n)])
        lo_first = jnp.concatenate([x, other], axis=dim)
        hi_first = jnp.concatenate([other, x], axis=dim)
        x = jnp.where(bit == 0, lo_first, hi_first)
    return x


def _nt(a, b):
    return lax.dot_general(a, b, (((1,), (1,)), ((), ())), preferred_element_type=F32)


def forward_kernel(x_ref, m_ref, s3_ref, s2_ref, s1_ref, y_ref, *col):
    j = pl.program_id(1)
    k = s1_ref.shape[0]
    x = x_ref[...] * m_ref[0]
    x1, x2, x3 = split(x)
    a = _nt(x1, s3_ref[...])
    c = _nt(x2, s2_ref[...])
    d = _nt(x3, s1_ref[...])
    part = ((a[:, 2 * k:] + c[:, k:] + d) + (a[:, k:2 * k] + c[:, :k])) + a[:, :k]

    @pl.when(j == 0)
    def _():
        y_ref[...] = part

    @pl.when(j > 0)
    def _():
        y_ref[...] += part

    if col:
        (c_ref,) = col
        i = pl.program_id(0)
        tw = x_ref.shape[1]
        s = jnp.sum(x, axis=0, keepdims=True)
        sl = pl.ds(pl.multiple_of(j * tw, tw), tw)

        @pl.when(i == 0)
        def _():
            c_ref[:, sl] = s

        @pl.when(i > 0)
        def _():
            c_ref[:, sl] += s


def backward_kernel(x_ref, m_ref, s3_ref, s2_ref, s1_ref, o_ref):
    i = pl.program_id(1)
    k = s1_ref.shape[0]
    x = x_ref[...] * m_ref[0]
    x1, x2, x3 = split(x)
    a = jnp.dot(s3_ref[...], x1, preferred_element_type=F32)
    c = jnp.dot(s2_ref[...], x2, preferred_element_type=F32)
    d = jnp.dot(s1_ref[...], x3, preferred_element_type=F32)
    part = ((a[2 * k:] + c[k:] + d) + (a[k:2 * k] + c[:k])) + a[:k]

    @pl.when(i == 0)
    def _():
        o_ref[...] = part

    @pl.when(i > 0)
    def _():
        o_ref[...] += part


def blocks(rows, width):
    tr = TILE
    tw = min(width, 4096)
    return tr, tw


def forward(expression, mexp, bt, with_colsum):
    rows, width = expression.shape
    k = bt.shape[0]
    tr, tw = blocks(rows, width)
    s3, s2, s1 = stacks(split_outside(bt), 0)
    in_specs = [
        pl.BlockSpec((tr, tw), lambda i, j: (i, j)),
        pl.BlockSpec((1, 1, tw), lambda i, j: (i, 0, j)),
        pl.BlockSpec((3 * k, tw), lambda i, j: (0, j)),
        pl.BlockSpec((2 * k, tw), lambda i, j: (0, j)),
        pl.BlockSpec((k, tw), lambda i, j: (0, j)),
    ]
    out_specs = [pl.BlockSpec((tr, k), lambda i, j: (i, 0))]
    out_shape = [jax.ShapeDtypeStruct((rows, k), F32)]
    if with_colsum:
        out_specs.append(pl.BlockSpec((1, width), lambda i, j: (0, 0)))
        out_shape.append(jax.ShapeDtypeStruct((1, width), F32))
    return pl.pallas_call(
        forward_kernel,
        grid=(rows // tr, width // tw),
        in_specs=in_specs,
        out_specs=out_specs,
        out_shape=out_shape,
        compiler_params=pltpu.CompilerParams(dimension_semantics=("arbitrary", "arbitrary")),
    )(expression, mexp, s3, s2, s1)


def backward(expression, mexp, y):
    rows, width = expression.shape
    k = y.shape[1]
    tr, tw = blocks(rows, width)
    s3, s2, s1 = stacks(split_outside(jnp.transpose(y)), 0)
    return pl.pallas_call(
        backward_kernel,
        grid=(width // tw, rows // tr),
        in_specs=[
            pl.BlockSpec((tr, tw), lambda j, i: (i, j)),
            pl.BlockSpec((1, 1, tw), lambda j, i: (i, 0, j)),
            pl.BlockSpec((3 * k, tr), lambda j, i: (0, i)),
            pl.BlockSpec((2 * k, tr), lambda j, i: (0, i)),
            pl.BlockSpec((k, tr), lambda j, i: (0, i)),
        ],
        out_specs=pl.BlockSpec((k, tw), lambda j, i: (0, j)),
        out_shape=jax.ShapeDtypeStruct((k, width), F32),
        compiler_params=pltpu.CompilerParams(dimension_semantics=("arbitrary", "arbitrary")),
    )(expression, mexp, s3, s2, s1)


HI = lax.Precision.HIGHEST


def row_gram(a, b):
    return lax.dot_general(a, b, (((1,), (1,)), ((), ())), precision=HI, preferred_element_type=F32)


def left_solve(lower, x):
    return lax.linalg.triangular_solve(lower, x, left_side=True, lower=True)


def right_solve(lower, x):
    return lax.linalg.triangular_solve(lower, x, left_side=False, lower=True, transpose_a=True)


def per_device(expression, tile_mask, start):
    cell_count = lax.axis_size("cell")
    gene_count = lax.axis_size("gene")
    rows, width = expression.shape
    cells = rows * cell_count

    mexp = jnp.repeat(tile_mask.astype(F32), TILE, axis=1)[:, None, :]
    start_t = jnp.transpose(start)
    gram0 = butterfly_sum(row_gram(start_t, start_t), "gene")
    lower0 = jnp.linalg.cholesky(gram0)
    current = left_solve(lower0, start_t)

    y_start, colsum = forward(expression, mexp, start_t, True)
    means = butterfly_sum(colsum[0], "cell") / cells
    y = right_solve(lower0, butterfly_sum(y_start, "gene"))

    older = None
    alpha_list = []
    beta_list = []
    for step in range(STEPS):
        if step > 0:
            y = butterfly_sum(forward(expression, mexp, current, False)[0], "gene")
        mean_side = butterfly_sum(jnp.dot(current, means, precision=HI), "gene")
        raw = halving_sum(backward(expression, mexp, y), "cell", 1)
        image = raw / cells - mean_side[:, None] * means[None, :]
        proj = [row_gram(current, image)]
        if older is not None:
            proj.append(row_gram(older, image))
        summed = butterfly_sum(jnp.stack(proj), "gene")
        resid = image - jnp.dot(jnp.transpose(summed[0]), current, precision=HI)
        if older is not None:
            resid = resid - jnp.dot(jnp.transpose(summed[1]), older, precision=HI)
        g = butterfly_sum(row_gram(resid, resid), "gene")
        lower = jnp.linalg.cholesky(g)
        fresh = left_solve(lower, resid)
        alpha_list.append(summed[0])
        beta_list.append(jnp.transpose(lower))
        older = current
        current = fresh
    next_block = jnp.transpose(current) * math.sqrt(width * gene_count)
    return (jnp.stack(alpha_list), jnp.stack(beta_list), next_block)


def solution(mesh):
    in_specs = (P("cell", "gene"), P("cell", "gene"), P("gene", None))
    out_specs = (P(), P(), P("gene", None))
    return jax.shard_map(
        per_device, mesh=mesh, in_specs=in_specs, out_specs=out_specs, check_vma=False
    )
```

```python
import math

import jax
import jax.numpy as jnp
from jax import lax
from jax.experimental import pallas as pl
from jax.experimental.pallas import tpu as pltpu
from jax.sharding import PartitionSpec as P

TILE = 256
STEPS = 2
BF = jnp.bfloat16
F32 = jnp.float32


def split(x):
    p1 = x.astype(BF)
    r1 = x - p1.astype(F32)
    p2 = r1.astype(BF)
    p3 = (r1 - p2.astype(F32)).astype(BF)
    return p1, p2, p3


def split_outside(x):
    pieces = []
    rest = x
    for _ in range(2):
        t = rest * 65537.0
        head = t - (t - rest)
        pieces.append(head.astype(BF))
        rest = rest - head
    pieces.append(rest.astype(BF))
    return pieces


def stacks(p, axis):
    return (jnp.concatenate(p, axis=axis), jnp.concatenate(p[:2], axis=axis), p[0])


def butterfly_sum(x, axis):
    n = lax.axis_size(axis)
    if n & (n - 1):
        return lax.psum(x, axis)
    s = 1
    while s < n:
        x = x + lax.ppermute(x, axis, [(i, i ^ s) for i in range(n)])
        s *= 2
    return x


def halving_sum(x, axis, dim):
    n = lax.axis_size(axis)
    if n & (n - 1) or x.shape[dim] % n:
        return lax.psum(x, axis)
    me = lax.axis_index(axis)
    levels = max(n.bit_length() - 2, 0)
    s = 1
    bits = []
    for _ in range(levels):
        half = x.shape[dim] // 2
        bit = (me // s) % 2
        keep = lax.dynamic_slice_in_dim(x, bit * half, half, axis=dim)
        send = lax.dynamic_slice_in_dim(x, (1 - bit) * half, half, axis=dim)
        x = keep + lax.ppermute(send, axis, [(i, i ^ s) for i in range(n)])
        bits.append((s, bit))
        s *= 2
    while s < n:
        x = x + lax.ppermute(x, axis, [(i, i ^ s) for i in range(n)])
        s *= 2
    for s, bit in reversed(bits):
        other = lax.ppermute(x, axis, [(i, i ^ s) for i in range(n)])
        lo_first = jnp.concatenate([x, other], axis=dim)
        hi_first = jnp.concatenate([other, x], axis=dim)
        x = jnp.where(bit == 0, lo_first, hi_first)
    return x


def _nt(a, b):
    return lax.dot_general(a, b, (((1,), (1,)), ((), ())), preferred_element_type=F32)


def forward_kernel(x_ref, m_ref, s3_ref, s2_ref, s1_ref, y_ref, *col):
    j = pl.program_id(1)
    k = s1_ref.shape[0]
    x = x_ref[...] * m_ref[0]
    x1, x2, x3 = split(x)
    a = _nt(x1, s3_ref[...])
    c = _nt(x2, s2_ref[...])
    d = _nt(x3, s1_ref[...])
    part = ((a[:, 2 * k:] + c[:, k:] + d) + (a[:, k:2 * k] + c[:, :k])) + a[:, :k]

    @pl.when(j == 0)
    def _():
        y_ref[...] = part

    @pl.when(j > 0)
    def _():
        y_ref[...] += part

    if col:
        (c_ref,) = col
        i = pl.program_id(0)
        tw = x_ref.shape[1]
        s = jnp.sum(x, axis=0, keepdims=True)
        sl = pl.ds(pl.multiple_of(j * tw, tw), tw)

        @pl.when(i == 0)
        def _():
            c_ref[:, sl] = s

        @pl.when(i > 0)
        def _():
            c_ref[:, sl] += s


def backward_kernel(x_ref, m_ref, s3_ref, s2_ref, s1_ref, o_ref):
    i = pl.program_id(1)
    k = s1_ref.shape[0]
    x = x_ref[...] * m_ref[0]
    x1, x2, x3 = split(x)
    a = jnp.dot(s3_ref[...], x1, preferred_element_type=F32)
    c = jnp.dot(s2_ref[...], x2, preferred_element_type=F32)
    d = jnp.dot(s1_ref[...], x3, preferred_element_type=F32)
    part = ((a[2 * k:] + c[k:] + d) + (a[k:2 * k] + c[:k])) + a[:k]

    @pl.when(i == 0)
    def _():
        o_ref[...] = part

    @pl.when(i > 0)
    def _():
        o_ref[...] += part


def blocks(rows, width):
    tr = TILE
    tw = min(width, 4096)
    return tr, tw


def forward(expression, mexp, bt, with_colsum):
    rows, width = expression.shape
    k = bt.shape[0]
    tr, tw = blocks(rows, width)
    s3, s2, s1 = stacks(split_outside(bt), 0)
    in_specs = [
        pl.BlockSpec((tr, tw), lambda i, j: (i, j)),
        pl.BlockSpec((1, 1, tw), lambda i, j: (i, 0, j)),
        pl.BlockSpec((3 * k, tw), lambda i, j: (0, j)),
        pl.BlockSpec((2 * k, tw), lambda i, j: (0, j)),
        pl.BlockSpec((k, tw), lambda i, j: (0, j)),
    ]
    out_specs = [pl.BlockSpec((tr, k), lambda i, j: (i, 0))]
    out_shape = [jax.ShapeDtypeStruct((rows, k), F32)]
    if with_colsum:
        out_specs.append(pl.BlockSpec((1, width), lambda i, j: (0, 0)))
        out_shape.append(jax.ShapeDtypeStruct((1, width), F32))
    return pl.pallas_call(
        forward_kernel,
        grid=(rows // tr, width // tw),
        in_specs=in_specs,
        out_specs=out_specs,
        out_shape=out_shape,
        compiler_params=pltpu.CompilerParams(dimension_semantics=("arbitrary", "arbitrary")),
    )(expression, mexp, s3, s2, s1)


def backward(expression, mexp, y):
    rows, width = expression.shape
    k = y.shape[1]
    tr, tw = blocks(rows, width)
    s3, s2, s1 = stacks(split_outside(jnp.transpose(y)), 0)
    return pl.pallas_call(
        backward_kernel,
        grid=(width // tw, rows // tr),
        in_specs=[
            pl.BlockSpec((tr, tw), lambda j, i: (i, j)),
            pl.BlockSpec((1, 1, tw), lambda j, i: (i, 0, j)),
            pl.BlockSpec((3 * k, tr), lambda j, i: (0, i)),
            pl.BlockSpec((2 * k, tr), lambda j, i: (0, i)),
            pl.BlockSpec((k, tr), lambda j, i: (0, i)),
        ],
        out_specs=pl.BlockSpec((k, tw), lambda j, i: (0, j)),
        out_shape=jax.ShapeDtypeStruct((k, width), F32),
        compiler_params=pltpu.CompilerParams(dimension_semantics=("arbitrary", "arbitrary")),
    )(expression, mexp, s3, s2, s1)


HI = lax.Precision.HIGHEST


def row_gram(a, b):
    return lax.dot_general(a, b, (((1,), (1,)), ((), ())), precision=HI, preferred_element_type=F32)


def left_solve(lower, x):
    return lax.linalg.triangular_solve(lower, x, left_side=True, lower=True)


def right_solve(lower, x):
    return lax.linalg.triangular_solve(lower, x, left_side=False, lower=True, transpose_a=True)


def per_device(expression, tile_mask, start):
    cell_count = lax.axis_size("cell")
    gene_count = lax.axis_size("gene")
    rows, width = expression.shape
    cells = rows * cell_count
    mexp = jnp.repeat(tile_mask.astype(F32), TILE, axis=1)[:, None, :]
    start_t = jnp.transpose(start)

    y_start, colsum = forward(expression, mexp, start_t, True)
    start_t = lax.optimization_barrier((start_t, y_start))[0]
    gram0 = butterfly_sum(row_gram(start_t, start_t), "gene")
    lower0 = jnp.linalg.cholesky(gram0)
    current = left_solve(lower0, start_t)
    means = butterfly_sum(colsum[0], "cell") / cells
    y = right_solve(lower0, butterfly_sum(y_start, "gene"))

    older = None
    older_side = None
    alpha_list = []
    beta_list = []
    for step in range(STEPS):
        if step > 0:
            y = butterfly_sum(forward(expression, mexp, current, False)[0], "gene")
        mean_side = butterfly_sum(jnp.dot(current, means, precision=HI), "gene")
        part = backward(expression, mexp, y)
        basis = [current] if older is None else [current, older]
        sides = [mean_side] if older is None else [mean_side, older_side]
        proj_part = jnp.stack([row_gram(v, part) for v in basis])
        proj_raw = butterfly_sum(butterfly_sum(proj_part, "cell"), "gene")
        raw = halving_sum(part, "cell", 1)
        image = raw / cells - mean_side[:, None] * means[None, :]
        summed = [proj_raw[t] / cells - sides[t][:, None] * mean_side[None, :] for t in range(len(basis))]
        resid = image - jnp.dot(jnp.transpose(summed[0]), current, precision=HI)
        if older is not None:
            resid = resid - jnp.dot(jnp.transpose(summed[1]), older, precision=HI)
        g = butterfly_sum(row_gram(resid, resid), "gene")
        lower = jnp.linalg.cholesky(g)
        fresh = left_solve(lower, resid)
        alpha_list.append(summed[0])
        beta_list.append(jnp.transpose(lower))
        older = current
        older_side = mean_side
        current = fresh
    next_block = jnp.transpose(current) * math.sqrt(width * gene_count)
    return (jnp.stack(alpha_list), jnp.stack(beta_list), next_block)


def solution(mesh):
    in_specs = (P("cell", "gene"), P("cell", "gene"), P("gene", None))
    out_specs = (P(), P(), P("gene", None))
    return jax.shard_map(
        per_device, mesh=mesh, in_specs=in_specs, out_specs=out_specs, check_vma=False
    )
```

```python
import math

import jax
import jax.numpy as jnp
from jax import lax
from jax.experimental import pallas as pl
from jax.experimental.pallas import tpu as pltpu
from jax.sharding import PartitionSpec as P

TILE = 256
STEPS = 2
BF = jnp.bfloat16
F32 = jnp.float32


def split(x):
    p1 = x.astype(BF)
    r1 = x - p1.astype(F32)
    p2 = r1.astype(BF)
    p3 = (r1 - p2.astype(F32)).astype(BF)
    return p1, p2, p3


def split_outside(x):
    pieces = []
    rest = x
    for _ in range(2):
        t = rest * 65537.0
        head = t - (t - rest)
        pieces.append(head.astype(BF))
        rest = rest - head
    pieces.append(rest.astype(BF))
    return pieces


def stacks(p, axis):
    return (jnp.concatenate(p, axis=axis), jnp.concatenate(p[:2], axis=axis), p[0])


def butterfly_sum(x, axis):
    n = lax.axis_size(axis)
    if n & (n - 1):
        return lax.psum(x, axis)
    s = 1
    while s < n:
        x = x + lax.ppermute(x, axis, [(i, i ^ s) for i in range(n)])
        s *= 2
    return x


def halving_sum(x, axis, dim):
    n = lax.axis_size(axis)
    if n & (n - 1) or x.shape[dim] % n:
        return lax.psum(x, axis)
    me = lax.axis_index(axis)
    levels = max(n.bit_length() - 2, 0)
    s = 1
    bits = []
    for _ in range(levels):
        half = x.shape[dim] // 2
        bit = (me // s) % 2
        keep = lax.dynamic_slice_in_dim(x, bit * half, half, axis=dim)
        send = lax.dynamic_slice_in_dim(x, (1 - bit) * half, half, axis=dim)
        x = keep + lax.ppermute(send, axis, [(i, i ^ s) for i in range(n)])
        bits.append((s, bit))
        s *= 2
    while s < n:
        x = x + lax.ppermute(x, axis, [(i, i ^ s) for i in range(n)])
        s *= 2
    for s, bit in reversed(bits):
        other = lax.ppermute(x, axis, [(i, i ^ s) for i in range(n)])
        lo_first = jnp.concatenate([x, other], axis=dim)
        hi_first = jnp.concatenate([other, x], axis=dim)
        x = jnp.where(bit == 0, lo_first, hi_first)
    return x


def pack_rows(x, extra):
    w = x.shape[1]
    flat = extra.reshape(-1)
    rows = -(-flat.shape[0] // w)
    flat = jnp.pad(flat, (0, rows * w - flat.shape[0]))
    return jnp.concatenate([x, flat.reshape(rows, w)], axis=0)


def unpack_rows(x, r, extra_shape):
    size = math.prod(extra_shape)
    return x[:r], x[r:].reshape(-1)[:size].reshape(extra_shape)


def gene_sum_with(x, extra):
    r = x.shape[0]
    return unpack_rows(butterfly_sum(pack_rows(x, extra), "gene"), r, extra.shape)


def cell_image_sum(part, extra):
    axis = "cell"
    n = lax.axis_size(axis)
    if n & (n - 1) or part.shape[1] % n:
        return lax.psum(part, axis), lax.psum(extra, axis)
    me = lax.axis_index(axis)
    levels = max(n.bit_length() - 2, 0)
    k = part.shape[0]
    x = part
    s = 1
    bits = []
    for _ in range(levels):
        half = x.shape[1] // 2
        bit = (me // s) % 2
        keep = lax.dynamic_slice_in_dim(x, bit * half, half, axis=1)
        send = lax.dynamic_slice_in_dim(x, (1 - bit) * half, half, axis=1)
        got = lax.ppermute(pack_rows(send, extra), axis, [(i, i ^ s) for i in range(n)])
        got_x, got_e = unpack_rows(got, k, extra.shape)
        x = keep + got_x
        extra = extra + got_e
        bits.append((s, bit))
        s *= 2
    while s < n:
        got = lax.ppermute(pack_rows(x, extra), axis, [(i, i ^ s) for i in range(n)])
        got_x, got_e = unpack_rows(got, k, extra.shape)
        x = x + got_x
        extra = extra + got_e
        s *= 2
    for s, bit in reversed(bits):
        other = lax.ppermute(x, axis, [(i, i ^ s) for i in range(n)])
        lo_first = jnp.concatenate([x, other], axis=1)
        hi_first = jnp.concatenate([other, x], axis=1)
        x = jnp.where(bit == 0, lo_first, hi_first)
    return x, extra


def _nt(a, b):
    return lax.dot_general(a, b, (((1,), (1,)), ((), ())), preferred_element_type=F32)


def forward_kernel(x_ref, m_ref, s3_ref, s2_ref, s1_ref, y_ref, *col):
    j = pl.program_id(1)
    k = s1_ref.shape[0]
    x = x_ref[...] * m_ref[0]
    x1, x2, x3 = split(x)
    a = _nt(x1, s3_ref[...])
    c = _nt(x2, s2_ref[...])
    d = _nt(x3, s1_ref[...])
    part = ((a[:, 2 * k:] + c[:, k:] + d) + (a[:, k:2 * k] + c[:, :k])) + a[:, :k]

    @pl.when(j == 0)
    def _():
        y_ref[...] = part

    @pl.when(j > 0)
    def _():
        y_ref[...] += part

    if col:
        (c_ref,) = col
        i = pl.program_id(0)
        tw = x_ref.shape[1]
        s = jnp.sum(x, axis=0, keepdims=True)
        sl = pl.ds(pl.multiple_of(j * tw, tw), tw)

        @pl.when(i == 0)
        def _():
            c_ref[:, sl] = s

        @pl.when(i > 0)
        def _():
            c_ref[:, sl] += s


def backward_kernel(x_ref, m_ref, s3_ref, s2_ref, s1_ref, o_ref):
    i = pl.program_id(1)
    k = s1_ref.shape[0]
    x = x_ref[...] * m_ref[0]
    x1, x2, x3 = split(x)
    a = jnp.dot(s3_ref[...], x1, preferred_element_type=F32)
    c = jnp.dot(s2_ref[...], x2, preferred_element_type=F32)
    d = jnp.dot(s1_ref[...], x3, preferred_element_type=F32)
    part = ((a[2 * k:] + c[k:] + d) + (a[k:2 * k] + c[:k])) + a[:k]

    @pl.when(i == 0)
    def _():
        o_ref[...] = part

    @pl.when(i > 0)
    def _():
        o_ref[...] += part


def blocks(rows, width):
    tr = TILE
    tw = min(width, 4096)
    return tr, tw


def forward(expression, mexp, bt, with_colsum):
    rows, width = expression.shape
    k = bt.shape[0]
    tr, tw = blocks(rows, width)
    s3, s2, s1 = stacks(split_outside(bt), 0)
    in_specs = [
        pl.BlockSpec((tr, tw), lambda i, j: (i, j)),
        pl.BlockSpec((1, 1, tw), lambda i, j: (i, 0, j)),
        pl.BlockSpec((3 * k, tw), lambda i, j: (0, j)),
        pl.BlockSpec((2 * k, tw), lambda i, j: (0, j)),
        pl.BlockSpec((k, tw), lambda i, j: (0, j)),
    ]
    out_specs = [pl.BlockSpec((tr, k), lambda i, j: (i, 0))]
    out_shape = [jax.ShapeDtypeStruct((rows, k), F32)]
    if with_colsum:
        out_specs.append(pl.BlockSpec((1, width), lambda i, j: (0, 0)))
        out_shape.append(jax.ShapeDtypeStruct((1, width), F32))
    return pl.pallas_call(
        forward_kernel,
        grid=(rows // tr, width // tw),
        in_specs=in_specs,
        out_specs=out_specs,
        out_shape=out_shape,
        compiler_params=pltpu.CompilerParams(dimension_semantics=("arbitrary", "arbitrary")),
    )(expression, mexp, s3, s2, s1)


def backward(expression, mexp, y):
    rows, width = expression.shape
    k = y.shape[1]
    tr, tw = blocks(rows, width)
    s3, s2, s1 = stacks(split_outside(jnp.transpose(y)), 0)
    return pl.pallas_call(
        backward_kernel,
        grid=(width // tw, rows // tr),
        in_specs=[
            pl.BlockSpec((tr, tw), lambda j, i: (i, j)),
            pl.BlockSpec((1, 1, tw), lambda j, i: (i, 0, j)),
            pl.BlockSpec((3 * k, tr), lambda j, i: (0, i)),
            pl.BlockSpec((2 * k, tr), lambda j, i: (0, i)),
            pl.BlockSpec((k, tr), lambda j, i: (0, i)),
        ],
        out_specs=pl.BlockSpec((k, tw), lambda j, i: (0, j)),
        out_shape=jax.ShapeDtypeStruct((k, width), F32),
        compiler_params=pltpu.CompilerParams(dimension_semantics=("arbitrary", "arbitrary")),
    )(expression, mexp, s3, s2, s1)


HI = lax.Precision.HIGHEST


def row_gram(a, b):
    return lax.dot_general(a, b, (((1,), (1,)), ((), ())), precision=HI, preferred_element_type=F32)


def left_solve(lower, x):
    return lax.linalg.triangular_solve(lower, x, left_side=True, lower=True)


def right_solve(lower, x):
    return lax.linalg.triangular_solve(lower, x, left_side=False, lower=True, transpose_a=True)


def per_device(expression, tile_mask, start):
    cell_count = lax.axis_size("cell")
    gene_count = lax.axis_size("gene")
    rows, width = expression.shape
    cells = rows * cell_count
    mexp = jnp.repeat(tile_mask.astype(F32), TILE, axis=1)[:, None, :]
    start_t = jnp.transpose(start)

    y_start, colsum = forward(expression, mexp, start_t, True)
    start_t = lax.optimization_barrier((start_t, y_start))[0]
    extra = jnp.concatenate([row_gram(start_t, start_t), jnp.sum(y_start, axis=0)[None, :]], axis=0)
    y_start, extra = gene_sum_with(y_start, extra)
    gram0 = extra[:-1]
    lower0 = jnp.linalg.cholesky(gram0)
    current = left_solve(lower0, start_t)
    y = right_solve(lower0, y_start)
    totals = butterfly_sum(jnp.concatenate([colsum[0], extra[-1]]), "cell")
    means = totals[:width] / cells
    mean_side = right_solve(lower0, (totals[width:] / cells)[None, :])[0]

    older = None
    older_side = None
    alpha_list = []
    beta_list = []
    for step in range(STEPS):
        if step > 0:
            y, mean_side = gene_sum_with(forward(expression, mexp, current, False)[0],
                                         jnp.dot(current, means, precision=HI))
        part = backward(expression, mexp, y)
        basis = [current] if older is None else [current, older]
        sides = [mean_side] if older is None else [mean_side, older_side]
        proj_part = jnp.stack([row_gram(v, part) for v in basis])
        raw, proj_cell = cell_image_sum(part, proj_part)
        proj_raw = butterfly_sum(proj_cell, "gene")
        image = raw / cells - mean_side[:, None] * means[None, :]
        summed = [proj_raw[t] / cells - sides[t][:, None] * mean_side[None, :] for t in range(len(basis))]
        resid = image - jnp.dot(jnp.transpose(summed[0]), current, precision=HI)
        if older is not None:
            resid = resid - jnp.dot(jnp.transpose(summed[1]), older, precision=HI)
        g = butterfly_sum(row_gram(resid, resid), "gene")
        lower = jnp.linalg.cholesky(g)
        fresh = left_solve(lower, resid)
        alpha_list.append(summed[0])
        beta_list.append(jnp.transpose(lower))
        older = current
        older_side = mean_side
        current = fresh
    next_block = jnp.transpose(current) * math.sqrt(width * gene_count)
    return (jnp.stack(alpha_list), jnp.stack(beta_list), next_block)


def solution(mesh):
    in_specs = (P("cell", "gene"), P("cell", "gene"), P("gene", None))
    out_specs = (P(), P(), P("gene", None))
    return jax.shard_map(
        per_device, mesh=mesh, in_specs=in_specs, out_specs=out_specs, check_vma=False
    )
```

```python
import math

import jax
import jax.numpy as jnp
from jax import lax
from jax.experimental import pallas as pl
from jax.experimental.pallas import tpu as pltpu
from jax.sharding import PartitionSpec as P

TILE = 256
STEPS = 2
BF = jnp.bfloat16
F32 = jnp.float32


def split(x):
    p1 = x.astype(BF)
    r1 = x - p1.astype(F32)
    p2 = r1.astype(BF)
    p3 = (r1 - p2.astype(F32)).astype(BF)
    return p1, p2, p3


def split_outside(x):
    pieces = []
    rest = x
    for _ in range(2):
        t = rest * 65537.0
        head = t - (t - rest)
        pieces.append(head.astype(BF))
        rest = rest - head
    pieces.append(rest.astype(BF))
    return pieces


def stacks(p, axis):
    return (jnp.concatenate(p, axis=axis), jnp.concatenate(p[:2], axis=axis), p[0])


def butterfly_sum(x, axis):
    n = lax.axis_size(axis)
    if n & (n - 1):
        return lax.psum(x, axis)
    s = 1
    while s < n:
        x = x + lax.ppermute(x, axis, [(i, i ^ s) for i in range(n)])
        s *= 2
    return x


def halving_sum(x, axis, dim):
    n = lax.axis_size(axis)
    if n & (n - 1) or x.shape[dim] % n:
        return lax.psum(x, axis)
    me = lax.axis_index(axis)
    levels = max(n.bit_length() - 2, 0)
    s = 1
    bits = []
    for _ in range(levels):
        half = x.shape[dim] // 2
        bit = (me // s) % 2
        keep = lax.dynamic_slice_in_dim(x, bit * half, half, axis=dim)
        send = lax.dynamic_slice_in_dim(x, (1 - bit) * half, half, axis=dim)
        x = keep + lax.ppermute(send, axis, [(i, i ^ s) for i in range(n)])
        bits.append((s, bit))
        s *= 2
    while s < n:
        x = x + lax.ppermute(x, axis, [(i, i ^ s) for i in range(n)])
        s *= 2
    for s, bit in reversed(bits):
        other = lax.ppermute(x, axis, [(i, i ^ s) for i in range(n)])
        lo_first = jnp.concatenate([x, other], axis=dim)
        hi_first = jnp.concatenate([other, x], axis=dim)
        x = jnp.where(bit == 0, lo_first, hi_first)
    return x


def pack_rows(x, extra):
    w = x.shape[1]
    flat = extra.reshape(-1)
    rows = -(-flat.shape[0] // w)
    flat = jnp.pad(flat, (0, rows * w - flat.shape[0]))
    return jnp.concatenate([x, flat.reshape(rows, w)], axis=0)


def unpack_rows(x, r, extra_shape):
    size = math.prod(extra_shape)
    return x[:r], x[r:].reshape(-1)[:size].reshape(extra_shape)


def gene_sum_with(x, extra):
    r = x.shape[0]
    return unpack_rows(butterfly_sum(pack_rows(x, extra), "gene"), r, extra.shape)


def cell_image_sum(part, extra):
    axis = "cell"
    n = lax.axis_size(axis)
    if n & (n - 1) or part.shape[1] % n:
        return lax.psum(part, axis), lax.psum(extra, axis)
    me = lax.axis_index(axis)
    levels = max(n.bit_length() - 2, 0)
    k = part.shape[0]
    x = part
    s = 1
    bits = []
    for _ in range(levels):
        half = x.shape[1] // 2
        bit = (me // s) % 2
        keep = lax.dynamic_slice_in_dim(x, bit * half, half, axis=1)
        send = lax.dynamic_slice_in_dim(x, (1 - bit) * half, half, axis=1)
        got = lax.ppermute(pack_rows(send, extra), axis, [(i, i ^ s) for i in range(n)])
        got_x, got_e = unpack_rows(got, k, extra.shape)
        x = keep + got_x
        extra = extra + got_e
        bits.append((s, bit))
        s *= 2
    while s < n:
        got = lax.ppermute(pack_rows(x, extra), axis, [(i, i ^ s) for i in range(n)])
        got_x, got_e = unpack_rows(got, k, extra.shape)
        x = x + got_x
        extra = extra + got_e
        s *= 2
    for s, bit in reversed(bits):
        other = lax.ppermute(x, axis, [(i, i ^ s) for i in range(n)])
        lo_first = jnp.concatenate([x, other], axis=1)
        hi_first = jnp.concatenate([other, x], axis=1)
        x = jnp.where(bit == 0, lo_first, hi_first)
    return x, extra


def _nt(a, b):
    return lax.dot_general(a, b, (((1,), (1,)), ((), ())), preferred_element_type=F32)


def forward_kernel(x_ref, m_ref, s3_ref, s2_ref, s1_ref, y_ref, *col):
    j = pl.program_id(1)
    k = s1_ref.shape[0]
    x = x_ref[...] * m_ref[0]
    x1, x2, x3 = split(x)
    a = _nt(x1, s3_ref[...])
    c = _nt(x2, s2_ref[...])
    d = _nt(x3, s1_ref[...])
    part = ((a[:, 2 * k:] + c[:, k:] + d) + (a[:, k:2 * k] + c[:, :k])) + a[:, :k]

    @pl.when(j == 0)
    def _():
        y_ref[...] = part

    @pl.when(j > 0)
    def _():
        y_ref[...] += part

    if col:
        (c_ref,) = col
        i = pl.program_id(0)
        tw = x_ref.shape[1]
        s = jnp.sum(x, axis=0, keepdims=True)
        sl = pl.ds(pl.multiple_of(j * tw, tw), tw)

        @pl.when(i == 0)
        def _():
            c_ref[:, sl] = s

        @pl.when(i > 0)
        def _():
            c_ref[:, sl] += s


def backward_kernel(x_ref, m_ref, s3_ref, s2_ref, s1_ref, o_ref):
    i = pl.program_id(1)
    k = s1_ref.shape[0]
    x = x_ref[...] * m_ref[0]
    x1, x2, x3 = split(x)
    a = jnp.dot(s3_ref[...], x1, preferred_element_type=F32)
    c = jnp.dot(s2_ref[...], x2, preferred_element_type=F32)
    d = jnp.dot(s1_ref[...], x3, preferred_element_type=F32)
    part = ((a[2 * k:] + c[k:] + d) + (a[k:2 * k] + c[:k])) + a[:k]

    @pl.when(i == 0)
    def _():
        o_ref[...] = part

    @pl.when(i > 0)
    def _():
        o_ref[...] += part


def blocks(rows, width):
    tr = TILE
    tw = min(width, 4096)
    return tr, tw


def forward(expression, mexp, bt, with_colsum):
    rows, width = expression.shape
    k = bt.shape[0]
    tr, tw = blocks(rows, width)
    s3, s2, s1 = stacks(split_outside(bt), 0)
    in_specs = [
        pl.BlockSpec((tr, tw), lambda i, j: (i, j)),
        pl.BlockSpec((1, 1, tw), lambda i, j: (i, 0, j)),
        pl.BlockSpec((3 * k, tw), lambda i, j: (0, j)),
        pl.BlockSpec((2 * k, tw), lambda i, j: (0, j)),
        pl.BlockSpec((k, tw), lambda i, j: (0, j)),
    ]
    out_specs = [pl.BlockSpec((tr, k), lambda i, j: (i, 0))]
    out_shape = [jax.ShapeDtypeStruct((rows, k), F32)]
    if with_colsum:
        out_specs.append(pl.BlockSpec((1, width), lambda i, j: (0, 0)))
        out_shape.append(jax.ShapeDtypeStruct((1, width), F32))
    return pl.pallas_call(
        forward_kernel,
        grid=(rows // tr, width // tw),
        in_specs=in_specs,
        out_specs=out_specs,
        out_shape=out_shape,
        compiler_params=pltpu.CompilerParams(dimension_semantics=("arbitrary", "arbitrary")),
    )(expression, mexp, s3, s2, s1)


def backward(expression, mexp, yt):
    rows, width = expression.shape
    k = yt.shape[0]
    tr, tw = blocks(rows, width)
    s3, s2, s1 = stacks(split_outside(yt), 0)
    return pl.pallas_call(
        backward_kernel,
        grid=(width // tw, rows // tr),
        in_specs=[
            pl.BlockSpec((tr, tw), lambda j, i: (i, j)),
            pl.BlockSpec((1, 1, tw), lambda j, i: (i, 0, j)),
            pl.BlockSpec((3 * k, tr), lambda j, i: (0, i)),
            pl.BlockSpec((2 * k, tr), lambda j, i: (0, i)),
            pl.BlockSpec((k, tr), lambda j, i: (0, i)),
        ],
        out_specs=pl.BlockSpec((k, tw), lambda j, i: (0, j)),
        out_shape=jax.ShapeDtypeStruct((k, width), F32),
        compiler_params=pltpu.CompilerParams(dimension_semantics=("arbitrary", "arbitrary")),
    )(expression, mexp, s3, s2, s1)


HI = lax.Precision.HIGHEST


def row_gram(a, b):
    return lax.dot_general(a, b, (((1,), (1,)), ((), ())), precision=HI, preferred_element_type=F32)


def left_solve(lower, x):
    return lax.linalg.triangular_solve(lower, x, left_side=True, lower=True)


def right_solve(lower, x):
    return lax.linalg.triangular_solve(lower, x, left_side=False, lower=True, transpose_a=True)


def per_device(expression, tile_mask, start):
    cell_count = lax.axis_size("cell")
    gene_count = lax.axis_size("gene")
    rows, width = expression.shape
    cells = rows * cell_count
    mexp = jnp.repeat(tile_mask.astype(F32), TILE, axis=1)[:, None, :]
    start_t = jnp.transpose(start)

    y_start, colsum = forward(expression, mexp, start_t, True)
    start_t = lax.optimization_barrier((start_t, y_start))[0]
    y_start = jnp.transpose(y_start)
    extra = jnp.concatenate([row_gram(start_t, start_t), jnp.sum(y_start, axis=1)[None, :]], axis=0)
    y_start, extra = gene_sum_with(y_start, extra)
    gram0 = extra[:-1]
    lower0 = jnp.linalg.cholesky(gram0)
    current = left_solve(lower0, start_t)
    y = left_solve(lower0, y_start)
    totals = butterfly_sum(jnp.concatenate([colsum[0], extra[-1]]), "cell")
    means = totals[:width] / cells
    mean_side = right_solve(lower0, (totals[width:] / cells)[None, :])[0]

    older = None
    older_side = None
    alpha_list = []
    beta_list = []
    for step in range(STEPS):
        if step > 0:
            y, mean_side = gene_sum_with(jnp.transpose(forward(expression, mexp, current, False)[0]),
                                         jnp.dot(current, means, precision=HI))
        part = backward(expression, mexp, y)
        basis = [current] if older is None else [current, older]
        sides = [mean_side] if older is None else [mean_side, older_side]
        proj_part = jnp.stack([row_gram(v, part) for v in basis])
        raw, proj_cell = cell_image_sum(part, proj_part)
        proj_raw = butterfly_sum(proj_cell, "gene")
        image = raw / cells - mean_side[:, None] * means[None, :]
        summed = [proj_raw[t] / cells - sides[t][:, None] * mean_side[None, :] for t in range(len(basis))]
        resid = image - jnp.dot(jnp.transpose(summed[0]), current, precision=HI)
        if older is not None:
            resid = resid - jnp.dot(jnp.transpose(summed[1]), older, precision=HI)
        g = butterfly_sum(row_gram(resid, resid), "gene")
        lower = jnp.linalg.cholesky(g)
        fresh = left_solve(lower, resid)
        alpha_list.append(summed[0])
        beta_list.append(jnp.transpose(lower))
        older = current
        older_side = mean_side
        current = fresh
    next_block = jnp.transpose(current) * math.sqrt(width * gene_count)
    return (jnp.stack(alpha_list), jnp.stack(beta_list), next_block)


def solution(mesh):
    in_specs = (P("cell", "gene"), P("cell", "gene"), P("gene", None))
    out_specs = (P(), P(), P("gene", None))
    return jax.shard_map(
        per_device, mesh=mesh, in_specs=in_specs, out_specs=out_specs, check_vma=False
    )
```

```python
import math

import jax
import jax.numpy as jnp
from jax import lax
from jax.experimental import pallas as pl
from jax.experimental.pallas import tpu as pltpu
from jax.sharding import PartitionSpec as P

TILE = 256
STEPS = 2
BF = jnp.bfloat16
F32 = jnp.float32


def split(x):
    p1 = x.astype(BF)
    r1 = x - p1.astype(F32)
    p2 = r1.astype(BF)
    p3 = (r1 - p2.astype(F32)).astype(BF)
    return p1, p2, p3


def split_outside(x):
    pieces = []
    rest = x
    for _ in range(2):
        t = rest * 65537.0
        head = t - (t - rest)
        pieces.append(head.astype(BF))
        rest = rest - head
    pieces.append(rest.astype(BF))
    return pieces


def stacks(p, axis):
    return (jnp.concatenate(p, axis=axis), jnp.concatenate(p[:2], axis=axis), p[0])


def butterfly_sum(x, axis):
    n = lax.axis_size(axis)
    if n & (n - 1):
        return lax.psum(x, axis)
    s = 1
    while s < n:
        x = x + lax.ppermute(x, axis, [(i, i ^ s) for i in range(n)])
        s *= 2
    return x


def halving_sum(x, axis, dim):
    n = lax.axis_size(axis)
    if n & (n - 1) or x.shape[dim] % n:
        return lax.psum(x, axis)
    me = lax.axis_index(axis)
    levels = max(n.bit_length() - 2, 0)
    s = 1
    bits = []
    for _ in range(levels):
        half = x.shape[dim] // 2
        bit = (me // s) % 2
        keep = lax.dynamic_slice_in_dim(x, bit * half, half, axis=dim)
        send = lax.dynamic_slice_in_dim(x, (1 - bit) * half, half, axis=dim)
        x = keep + lax.ppermute(send, axis, [(i, i ^ s) for i in range(n)])
        bits.append((s, bit))
        s *= 2
    while s < n:
        x = x + lax.ppermute(x, axis, [(i, i ^ s) for i in range(n)])
        s *= 2
    for s, bit in reversed(bits):
        other = lax.ppermute(x, axis, [(i, i ^ s) for i in range(n)])
        lo_first = jnp.concatenate([x, other], axis=dim)
        hi_first = jnp.concatenate([other, x], axis=dim)
        x = jnp.where(bit == 0, lo_first, hi_first)
    return x


def pack_rows(x, extra):
    w = x.shape[1]
    flat = extra.reshape(-1)
    rows = -(-flat.shape[0] // w)
    flat = jnp.pad(flat, (0, rows * w - flat.shape[0]))
    return jnp.concatenate([x, flat.reshape(rows, w)], axis=0)


def unpack_rows(x, r, extra_shape):
    size = math.prod(extra_shape)
    return x[:r], x[r:].reshape(-1)[:size].reshape(extra_shape)


def gene_sum_with(x, extra):
    r = x.shape[0]
    return unpack_rows(butterfly_sum(pack_rows(x, extra), "gene"), r, extra.shape)


def cell_image_sum(part, extra):
    axis = "cell"
    n = lax.axis_size(axis)
    if n & (n - 1) or part.shape[1] % n:
        return lax.psum(part, axis), lax.psum(extra, axis)
    me = lax.axis_index(axis)
    levels = max(n.bit_length() - 2, 0)
    k = part.shape[0]
    x = part
    s = 1
    bits = []
    for _ in range(levels):
        half = x.shape[1] // 2
        bit = (me // s) % 2
        keep = lax.dynamic_slice_in_dim(x, bit * half, half, axis=1)
        send = lax.dynamic_slice_in_dim(x, (1 - bit) * half, half, axis=1)
        got = lax.ppermute(pack_rows(send, extra), axis, [(i, i ^ s) for i in range(n)])
        got_x, got_e = unpack_rows(got, k, extra.shape)
        x = keep + got_x
        extra = extra + got_e
        bits.append((s, bit))
        s *= 2
    while s < n:
        got = lax.ppermute(pack_rows(x, extra), axis, [(i, i ^ s) for i in range(n)])
        got_x, got_e = unpack_rows(got, k, extra.shape)
        x = x + got_x
        extra = extra + got_e
        s *= 2
    for s, bit in reversed(bits):
        other = lax.ppermute(x, axis, [(i, i ^ s) for i in range(n)])
        lo_first = jnp.concatenate([x, other], axis=1)
        hi_first = jnp.concatenate([other, x], axis=1)
        x = jnp.where(bit == 0, lo_first, hi_first)
    return x, extra


def _nt(a, b):
    return lax.dot_general(a, b, (((1,), (1,)), ((), ())), preferred_element_type=F32)


def forward_kernel(x_ref, m_ref, s3_ref, s2_ref, s1_ref, y_ref, *col):
    j = pl.program_id(1)
    k = s1_ref.shape[0]
    x = x_ref[...] * m_ref[0]
    x1, x2, x3 = split(x)
    a = _nt(x1, s3_ref[...])
    c = _nt(x2, s2_ref[...])
    d = _nt(x3, s1_ref[...])
    part = ((a[:, 2 * k:] + c[:, k:] + d) + (a[:, k:2 * k] + c[:, :k])) + a[:, :k]

    @pl.when(j == 0)
    def _():
        y_ref[...] = part

    @pl.when(j > 0)
    def _():
        y_ref[...] += part

    if col:
        (c_ref,) = col
        i = pl.program_id(0)
        tw = x_ref.shape[1]
        s = jnp.sum(x, axis=0, keepdims=True)
        sl = pl.ds(pl.multiple_of(j * tw, tw), tw)

        @pl.when(i == 0)
        def _():
            c_ref[:, sl] = s

        @pl.when(i > 0)
        def _():
            c_ref[:, sl] += s


def backward_kernel(x_ref, m_ref, s3_ref, s2_ref, s1_ref, *refs):
    i = pl.program_id(1)
    k = s1_ref.shape[0]
    x = x_ref[...] * m_ref[0]
    x1, x2, x3 = split(x)
    a = jnp.dot(s3_ref[...], x1, preferred_element_type=F32)
    c = jnp.dot(s2_ref[...], x2, preferred_element_type=F32)
    d = jnp.dot(s1_ref[...], x3, preferred_element_type=F32)
    part = ((a[2 * k:] + c[k:] + d) + (a[k:2 * k] + c[:k])) + a[:k]
    o_ref = refs[-1]

    @pl.when(i == 0)
    def _():
        if len(refs) == 2:
            o_ref[...] = refs[0][...] + part
        else:
            o_ref[...] = part

    @pl.when(i > 0)
    def _():
        o_ref[...] += part


def blocks(rows, width):
    tr = TILE
    tw = min(width, 4096)
    return tr, tw


def forward(expression, mexp, bt, with_colsum, lo, count):
    rows, width = expression.shape
    k = bt.shape[0]
    tr, tw = blocks(rows, width)
    off = lo // tr
    s3, s2, s1 = stacks(split_outside(bt), 0)
    in_specs = [
        pl.BlockSpec((tr, tw), lambda i, j: (i + off, j)),
        pl.BlockSpec((1, 1, tw), lambda i, j: (i + off, 0, j)),
        pl.BlockSpec((3 * k, tw), lambda i, j: (0, j)),
        pl.BlockSpec((2 * k, tw), lambda i, j: (0, j)),
        pl.BlockSpec((k, tw), lambda i, j: (0, j)),
    ]
    out_specs = [pl.BlockSpec((tr, k), lambda i, j: (i, 0))]
    out_shape = [jax.ShapeDtypeStruct((count, k), F32)]
    if with_colsum:
        out_specs.append(pl.BlockSpec((1, width), lambda i, j: (0, 0)))
        out_shape.append(jax.ShapeDtypeStruct((1, width), F32))
    return pl.pallas_call(
        forward_kernel,
        grid=(count // tr, width // tw),
        in_specs=in_specs,
        out_specs=out_specs,
        out_shape=out_shape,
        compiler_params=pltpu.CompilerParams(dimension_semantics=("arbitrary", "arbitrary")),
    )(expression, mexp, s3, s2, s1)


def backward(expression, mexp, yt, lo, init=None):
    rows, width = expression.shape
    k, count = yt.shape
    tr, tw = blocks(rows, width)
    off = lo // tr
    s3, s2, s1 = stacks(split_outside(yt), 0)
    in_specs = [
        pl.BlockSpec((tr, tw), lambda j, i: (i + off, j)),
        pl.BlockSpec((1, 1, tw), lambda j, i: (i + off, 0, j)),
        pl.BlockSpec((3 * k, tr), lambda j, i: (0, i)),
        pl.BlockSpec((2 * k, tr), lambda j, i: (0, i)),
        pl.BlockSpec((k, tr), lambda j, i: (0, i)),
    ]
    args = [expression, mexp, s3, s2, s1]
    if init is not None:
        in_specs.append(pl.BlockSpec((k, tw), lambda j, i: (0, j)))
        args.append(init)
    return pl.pallas_call(
        backward_kernel,
        grid=(width // tw, count // tr),
        in_specs=in_specs,
        out_specs=pl.BlockSpec((k, tw), lambda j, i: (0, j)),
        out_shape=jax.ShapeDtypeStruct((k, width), F32),
        compiler_params=pltpu.CompilerParams(dimension_semantics=("arbitrary", "arbitrary")),
    )(*args)


HI = lax.Precision.HIGHEST


def row_gram(a, b):
    return lax.dot_general(a, b, (((1,), (1,)), ((), ())), precision=HI, preferred_element_type=F32)


def left_solve(lower, x):
    return lax.linalg.triangular_solve(lower, x, left_side=True, lower=True)


def right_solve(lower, x):
    return lax.linalg.triangular_solve(lower, x, left_side=False, lower=True, transpose_a=True)


def row_halves(rows):
    tiles = rows // TILE
    first = (tiles + 1) // 2 * TILE
    return [(0, first), (first, rows - first)] if first < rows else [(0, rows)]


def per_device(expression, tile_mask, start):
    cell_count = lax.axis_size("cell")
    gene_count = lax.axis_size("gene")
    rows, width = expression.shape
    cells = rows * cell_count
    mexp = jnp.repeat(tile_mask.astype(F32), TILE, axis=1)[:, None, :]
    start_t = jnp.transpose(start)
    halves = row_halves(rows)

    ys = []
    colsum = 0.0
    row_total = 0.0
    for h, (lo, count) in enumerate(halves):
        y_h, c_h = forward(expression, mexp, start_t, True, lo, count)
        colsum = colsum + c_h[0]
        y_h = jnp.transpose(y_h)
        if h == 0:
            start_t = lax.optimization_barrier((start_t, y_h))[0]
            extra = jnp.concatenate([row_gram(start_t, start_t), jnp.sum(y_h, axis=1)[None, :]], axis=0)
            y_h, extra = gene_sum_with(y_h, extra)
            gram0 = extra[:-1]
            row_total = row_total + extra[-1]
        else:
            y_h, extra = gene_sum_with(y_h, jnp.sum(y_h, axis=1))
            row_total = row_total + extra
        ys.append(y_h)
    lower0 = jnp.linalg.cholesky(gram0)
    current = left_solve(lower0, start_t)
    ys = [left_solve(lower0, y_h) for y_h in ys]
    totals = butterfly_sum(jnp.concatenate([colsum, row_total]), "cell")
    means = totals[:width] / cells
    mean_side = right_solve(lower0, (totals[width:] / cells)[None, :])[0]

    older = None
    older_side = None
    alpha_list = []
    beta_list = []
    for step in range(STEPS):
        if step > 0:
            ys = []
            for h, (lo, count) in enumerate(halves):
                y_h = jnp.transpose(forward(expression, mexp, current, False, lo, count)[0])
                if h == 0:
                    y_h, mean_side = gene_sum_with(y_h, jnp.dot(current, means, precision=HI))
                else:
                    y_h = butterfly_sum(y_h, "gene")
                ys.append(y_h)
        part = None
        for (lo, count), y_h in zip(halves, ys):
            part = backward(expression, mexp, y_h, lo, part)
        basis = [current] if older is None else [current, older]
        sides = [mean_side] if older is None else [mean_side, older_side]
        proj_part = jnp.stack([row_gram(v, part) for v in basis])
        raw, proj_cell = cell_image_sum(part, proj_part)
        proj_raw = butterfly_sum(proj_cell, "gene")
        image = raw / cells - mean_side[:, None] * means[None, :]
        summed = [proj_raw[t] / cells - sides[t][:, None] * mean_side[None, :] for t in range(len(basis))]
        resid = image - jnp.dot(jnp.transpose(summed[0]), current, precision=HI)
        if older is not None:
            resid = resid - jnp.dot(jnp.transpose(summed[1]), older, precision=HI)
        g = butterfly_sum(row_gram(resid, resid), "gene")
        lower = jnp.linalg.cholesky(g)
        fresh = left_solve(lower, resid)
        alpha_list.append(summed[0])
        beta_list.append(jnp.transpose(lower))
        older = current
        older_side = mean_side
        current = fresh
    next_block = jnp.transpose(current) * math.sqrt(width * gene_count)
    return (jnp.stack(alpha_list), jnp.stack(beta_list), next_block)


def solution(mesh):
    in_specs = (P("cell", "gene"), P("cell", "gene"), P("gene", None))
    out_specs = (P(), P(), P("gene", None))
    return jax.shard_map(
        per_device, mesh=mesh, in_specs=in_specs, out_specs=out_specs, check_vma=False
    )
```

```python
import math

import jax
import jax.numpy as jnp
from jax import lax
from jax.experimental import pallas as pl
from jax.experimental.pallas import tpu as pltpu
from jax.sharding import PartitionSpec as P

TILE = 256
STEPS = 2
BF = jnp.bfloat16
F32 = jnp.float32


def split(x):
    p1 = x.astype(BF)
    r1 = x - p1.astype(F32)
    p2 = r1.astype(BF)
    p3 = (r1 - p2.astype(F32)).astype(BF)
    return p1, p2, p3


def butterfly_sum(x, axis):
    n = lax.axis_size(axis)
    if n & (n - 1):
        return lax.psum(x, axis)
    s = 1
    while s < n:
        x = x + lax.ppermute(x, axis, [(i, i ^ s) for i in range(n)])
        s *= 2
    return x


def halving_sum(x, axis, dim):
    n = lax.axis_size(axis)
    if n & (n - 1) or x.shape[dim] % n:
        return lax.psum(x, axis)
    me = lax.axis_index(axis)
    levels = max(n.bit_length() - 2, 0)
    s = 1
    bits = []
    for _ in range(levels):
        half = x.shape[dim] // 2
        bit = (me // s) % 2
        keep = lax.dynamic_slice_in_dim(x, bit * half, half, axis=dim)
        send = lax.dynamic_slice_in_dim(x, (1 - bit) * half, half, axis=dim)
        x = keep + lax.ppermute(send, axis, [(i, i ^ s) for i in range(n)])
        bits.append((s, bit))
        s *= 2
    while s < n:
        x = x + lax.ppermute(x, axis, [(i, i ^ s) for i in range(n)])
        s *= 2
    for s, bit in reversed(bits):
        other = lax.ppermute(x, axis, [(i, i ^ s) for i in range(n)])
        lo_first = jnp.concatenate([x, other], axis=dim)
        hi_first = jnp.concatenate([other, x], axis=dim)
        x = jnp.where(bit == 0, lo_first, hi_first)
    return x


def pack_rows(x, extra):
    w = x.shape[1]
    flat = extra.reshape(-1)
    rows = -(-flat.shape[0] // w)
    flat = jnp.pad(flat, (0, rows * w - flat.shape[0]))
    return jnp.concatenate([x, flat.reshape(rows, w)], axis=0)


def unpack_rows(x, r, extra_shape):
    size = math.prod(extra_shape)
    return x[:r], x[r:].reshape(-1)[:size].reshape(extra_shape)


def gene_sum_with(x, extra):
    r = x.shape[0]
    return unpack_rows(butterfly_sum(pack_rows(x, extra), "gene"), r, extra.shape)


def cell_image_sum(part, extra):
    axis = "cell"
    n = lax.axis_size(axis)
    if n & (n - 1) or part.shape[1] % n:
        return lax.psum(part, axis), lax.psum(extra, axis)
    me = lax.axis_index(axis)
    levels = max(n.bit_length() - 2, 0)
    k = part.shape[0]
    x = part
    s = 1
    bits = []
    for _ in range(levels):
        half = x.shape[1] // 2
        bit = (me // s) % 2
        keep = lax.dynamic_slice_in_dim(x, bit * half, half, axis=1)
        send = lax.dynamic_slice_in_dim(x, (1 - bit) * half, half, axis=1)
        got = lax.ppermute(pack_rows(send, extra), axis, [(i, i ^ s) for i in range(n)])
        got_x, got_e = unpack_rows(got, k, extra.shape)
        x = keep + got_x
        extra = extra + got_e
        bits.append((s, bit))
        s *= 2
    while s < n:
        got = lax.ppermute(pack_rows(x, extra), axis, [(i, i ^ s) for i in range(n)])
        got_x, got_e = unpack_rows(got, k, extra.shape)
        x = x + got_x
        extra = extra + got_e
        s *= 2
    for s, bit in reversed(bits):
        other = lax.ppermute(x, axis, [(i, i ^ s) for i in range(n)])
        lo_first = jnp.concatenate([x, other], axis=1)
        hi_first = jnp.concatenate([other, x], axis=1)
        x = jnp.where(bit == 0, lo_first, hi_first)
    return x, extra


def _nt(a, b):
    return lax.dot_general(a, b, (((1,), (1,)), ((), ())), preferred_element_type=F32)


def _masked(x_ref, m_ref):
    tr, tw = x_ref.shape
    x = x_ref[...].reshape(tr // TILE, TILE, tw) * m_ref[...]
    return x.reshape(tr, tw)


def _pieces(v_ref):
    p = split(v_ref[...])
    return jnp.concatenate(p, axis=0), jnp.concatenate(p[:2], axis=0), p[0]


def forward_kernel(x_ref, m_ref, v_ref, y_ref, *col):
    j = pl.program_id(1)
    k = v_ref.shape[0]
    x = _masked(x_ref, m_ref)
    x1, x2, x3 = split(x)
    s3, s2, s1 = _pieces(v_ref)
    a = _nt(s3, x1)
    c = _nt(s2, x2)
    d = _nt(s1, x3)
    part = ((a[2 * k:] + c[k:] + d) + (a[k:2 * k] + c[:k])) + a[:k]

    @pl.when(j == 0)
    def _():
        y_ref[...] = part

    @pl.when(j > 0)
    def _():
        y_ref[...] += part

    if col:
        (c_ref,) = col
        i = pl.program_id(0)
        tw = x_ref.shape[1]
        s = jnp.sum(x, axis=0, keepdims=True)
        sl = pl.ds(pl.multiple_of(j * tw, tw), tw)

        @pl.when(i == 0)
        def _():
            c_ref[:, sl] = s

        @pl.when(i > 0)
        def _():
            c_ref[:, sl] += s


def backward_kernel(x_ref, m_ref, v_ref, o_ref, *col):
    i = pl.program_id(1)
    k = v_ref.shape[0]
    x = _masked(x_ref, m_ref)
    x1, x2, x3 = split(x)
    p = split(v_ref[...])
    ones = [jnp.ones((8, v_ref.shape[1]), BF)] if col else []
    a = jnp.dot(jnp.concatenate(list(p) + ones, axis=0), x1, preferred_element_type=F32)
    c = jnp.dot(jnp.concatenate(list(p[:2]) + ones, axis=0), x2, preferred_element_type=F32)
    d = jnp.dot(jnp.concatenate(list(p[:1]) + ones, axis=0), x3, preferred_element_type=F32)
    part = ((a[2 * k:3 * k] + c[k:2 * k] + d[:k]) + (a[k:2 * k] + c[:k])) + a[:k]

    @pl.when(i == 0)
    def _():
        o_ref[...] = part

    @pl.when(i > 0)
    def _():
        o_ref[...] += part

    if col:
        (c_ref,) = col
        sums = (d[k:k + 1] + c[2 * k:2 * k + 1]) + a[3 * k:3 * k + 1]

        @pl.when(i == 0)
        def _():
            c_ref[...] = sums

        @pl.when(i > 0)
        def _():
            c_ref[...] += sums


def blocks(rows, width):
    tr = 2 * TILE if rows % (2 * TILE) == 0 else TILE
    tw = min(width, 4096)
    return tr, tw


def forward(expression, mexp, bt, with_colsum):
    rows, width = expression.shape
    k = bt.shape[0]
    tr, tw = blocks(rows, width)
    in_specs = [
        pl.BlockSpec((tr, tw), lambda i, j: (i, j)),
        pl.BlockSpec((tr // TILE, 1, tw), lambda i, j: (i, 0, j)),
        pl.BlockSpec((k, tw), lambda i, j: (0, j)),
    ]
    out_specs = [pl.BlockSpec((k, tr), lambda i, j: (0, i))]
    out_shape = [jax.ShapeDtypeStruct((k, rows), F32)]
    if with_colsum:
        out_specs.append(pl.BlockSpec((1, width), lambda i, j: (0, 0)))
        out_shape.append(jax.ShapeDtypeStruct((1, width), F32))
    return pl.pallas_call(
        forward_kernel,
        grid=(rows // tr, width // tw),
        in_specs=in_specs,
        out_specs=out_specs,
        out_shape=out_shape,
        compiler_params=pltpu.CompilerParams(dimension_semantics=("arbitrary", "arbitrary")),
    )(expression, mexp, bt)


def backward(expression, mexp, yt, with_colsum):
    rows, width = expression.shape
    k = yt.shape[0]
    tr, tw = blocks(rows, width)
    out_specs = [pl.BlockSpec((k, tw), lambda j, i: (0, j))]
    out_shape = [jax.ShapeDtypeStruct((k, width), F32)]
    if with_colsum:
        out_specs.append(pl.BlockSpec((1, tw), lambda j, i: (0, j)))
        out_shape.append(jax.ShapeDtypeStruct((1, width), F32))
    return pl.pallas_call(
        backward_kernel,
        grid=(width // tw, rows // tr),
        in_specs=[
            pl.BlockSpec((tr, tw), lambda j, i: (i, j)),
            pl.BlockSpec((tr // TILE, 1, tw), lambda j, i: (i, 0, j)),
            pl.BlockSpec((k, tr), lambda j, i: (0, i)),
        ],
        out_specs=out_specs,
        out_shape=out_shape,
        compiler_params=pltpu.CompilerParams(dimension_semantics=("arbitrary", "arbitrary")),
    )(expression, mexp, yt)


HI = lax.Precision.HIGHEST


def row_gram(a, b):
    return lax.dot_general(a, b, (((1,), (1,)), ((), ())), precision=HI, preferred_element_type=F32)


def left_solve(lower, x):
    return lax.linalg.triangular_solve(lower, x, left_side=True, lower=True)


def right_solve(lower, x):
    return lax.linalg.triangular_solve(lower, x, left_side=False, lower=True, transpose_a=True)


def per_device(expression, tile_mask, start):
    cell_count = lax.axis_size("cell")
    gene_count = lax.axis_size("gene")
    rows, width = expression.shape
    cells = rows * cell_count
    mexp = jnp.repeat(tile_mask.astype(F32), TILE, axis=1)[:, None, :]
    start_t = jnp.transpose(start)

    y_start = forward(expression, mexp, start_t, False)[0]
    start_t = lax.optimization_barrier((start_t, y_start))[0]
    extra = jnp.concatenate([row_gram(start_t, start_t), jnp.sum(y_start, axis=1)[None, :]], axis=0)
    y_start, extra = gene_sum_with(y_start, extra)
    gram0 = extra[:-1]
    row_total = extra[-1]
    lower0 = jnp.linalg.cholesky(gram0)
    current = left_solve(lower0, start_t)
    y = left_solve(lower0, y_start)

    older = None
    older_side = None
    alpha_list = []
    beta_list = []
    for step in range(STEPS):
        if step > 0:
            y, mean_side = gene_sum_with(forward(expression, mexp, current, False)[0],
                                         jnp.dot(current, means, precision=HI))
        basis = [current] if older is None else [current, older]
        if step == 0:
            part, colsum = backward(expression, mexp, y, True)
            proj_part = jnp.stack([row_gram(v, part) for v in basis])
            ride = jnp.concatenate([proj_part.reshape(-1), colsum[0], row_total])
            raw, ride = cell_image_sum(part, ride)
            proj_cell = ride[:proj_part.size].reshape(proj_part.shape)
            means = ride[proj_part.size:proj_part.size + width] / cells
            mean_side = right_solve(lower0, (ride[proj_part.size + width:] / cells)[None, :])[0]
        else:
            part = backward(expression, mexp, y, False)[0]
            proj_part = jnp.stack([row_gram(v, part) for v in basis])
            raw, proj_cell = cell_image_sum(part, proj_part)
        sides = [mean_side] if older is None else [mean_side, older_side]
        proj_raw = butterfly_sum(proj_cell, "gene")
        image = raw / cells - mean_side[:, None] * means[None, :]
        summed = [proj_raw[t] / cells - sides[t][:, None] * mean_side[None, :] for t in range(len(basis))]
        resid = image - jnp.dot(jnp.transpose(summed[0]), current, precision=HI)
        if older is not None:
            resid = resid - jnp.dot(jnp.transpose(summed[1]), older, precision=HI)
        g = butterfly_sum(row_gram(resid, resid), "gene")
        lower = jnp.linalg.cholesky(g)
        fresh = left_solve(lower, resid)
        alpha_list.append(summed[0])
        beta_list.append(jnp.transpose(lower))
        older = current
        older_side = mean_side
        current = fresh
    next_block = jnp.transpose(current) * math.sqrt(width * gene_count)
    return (jnp.stack(alpha_list), jnp.stack(beta_list), next_block)


def solution(mesh):
    in_specs = (P("cell", "gene"), P("cell", "gene"), P("gene", None))
    out_specs = (P(), P(), P("gene", None))
    return jax.shard_map(
        per_device, mesh=mesh, in_specs=in_specs, out_specs=out_specs, check_vma=False
    )
```

```python
import math

import jax
import jax.numpy as jnp
from jax import lax
from jax.experimental import pallas as pl
from jax.experimental.pallas import tpu as pltpu
from jax.sharding import PartitionSpec as P

TILE = 256
STEPS = 2
BF = jnp.bfloat16
F32 = jnp.float32


def split(x):
    p1 = x.astype(BF)
    r1 = x - p1.astype(F32)
    p2 = r1.astype(BF)
    p3 = (r1 - p2.astype(F32)).astype(BF)
    return p1, p2, p3


def butterfly_sum(x, axis):
    n = lax.axis_size(axis)
    if n & (n - 1):
        return lax.psum(x, axis)
    s = 1
    while s < n:
        x = x + lax.ppermute(x, axis, [(i, i ^ s) for i in range(n)])
        s *= 2
    return x


def halving_sum(x, axis, dim):
    n = lax.axis_size(axis)
    if n & (n - 1) or x.shape[dim] % n:
        return lax.psum(x, axis)
    me = lax.axis_index(axis)
    levels = max(n.bit_length() - 2, 0)
    s = 1
    bits = []
    for _ in range(levels):
        half = x.shape[dim] // 2
        bit = (me // s) % 2
        keep = lax.dynamic_slice_in_dim(x, bit * half, half, axis=dim)
        send = lax.dynamic_slice_in_dim(x, (1 - bit) * half, half, axis=dim)
        x = keep + lax.ppermute(send, axis, [(i, i ^ s) for i in range(n)])
        bits.append((s, bit))
        s *= 2
    while s < n:
        x = x + lax.ppermute(x, axis, [(i, i ^ s) for i in range(n)])
        s *= 2
    for s, bit in reversed(bits):
        other = lax.ppermute(x, axis, [(i, i ^ s) for i in range(n)])
        lo_first = jnp.concatenate([x, other], axis=dim)
        hi_first = jnp.concatenate([other, x], axis=dim)
        x = jnp.where(bit == 0, lo_first, hi_first)
    return x


def pack_rows(x, extra):
    w = x.shape[1]
    flat = extra.reshape(-1)
    rows = -(-flat.shape[0] // w)
    flat = jnp.pad(flat, (0, rows * w - flat.shape[0]))
    return jnp.concatenate([x, flat.reshape(rows, w)], axis=0)


def unpack_rows(x, r, extra_shape):
    size = math.prod(extra_shape)
    return x[:r], x[r:].reshape(-1)[:size].reshape(extra_shape)


def gene_sum_with(x, extra):
    r = x.shape[0]
    return unpack_rows(butterfly_sum(pack_rows(x, extra), "gene"), r, extra.shape)


def cell_image_sum(part, extra):
    axis = "cell"
    n = lax.axis_size(axis)
    if n & (n - 1) or part.shape[1] % n:
        return lax.psum(part, axis), lax.psum(extra, axis)
    me = lax.axis_index(axis)
    levels = max(n.bit_length() - 2, 0)
    k = part.shape[0]
    x = part
    s = 1
    bits = []
    for _ in range(levels):
        half = x.shape[1] // 2
        bit = (me // s) % 2
        keep = lax.dynamic_slice_in_dim(x, bit * half, half, axis=1)
        send = lax.dynamic_slice_in_dim(x, (1 - bit) * half, half, axis=1)
        got = lax.ppermute(pack_rows(send, extra), axis, [(i, i ^ s) for i in range(n)])
        got_x, got_e = unpack_rows(got, k, extra.shape)
        x = keep + got_x
        extra = extra + got_e
        bits.append((s, bit))
        s *= 2
    while s < n:
        got = lax.ppermute(pack_rows(x, extra), axis, [(i, i ^ s) for i in range(n)])
        got_x, got_e = unpack_rows(got, k, extra.shape)
        x = x + got_x
        extra = extra + got_e
        s *= 2
    for s, bit in reversed(bits):
        other = lax.ppermute(x, axis, [(i, i ^ s) for i in range(n)])
        lo_first = jnp.concatenate([x, other], axis=1)
        hi_first = jnp.concatenate([other, x], axis=1)
        x = jnp.where(bit == 0, lo_first, hi_first)
    return x, extra


def _nt(a, b):
    return lax.dot_general(a, b, (((1,), (1,)), ((), ())), preferred_element_type=F32)


def _masked(x_ref, m_ref):
    tr, tw = x_ref.shape
    x = x_ref[...].reshape(tr // TILE, TILE, tw) * m_ref[...]
    return x.reshape(tr, tw)


def _pieces(v_ref):
    p = split(v_ref[...])
    return jnp.concatenate(p, axis=0), jnp.concatenate(p[:2], axis=0), p[0]


def forward_kernel(x_ref, m_ref, v_ref, y_ref, *col):
    j = pl.program_id(1)
    k = v_ref.shape[0]
    x = _masked(x_ref, m_ref)
    x1, x2, x3 = split(x)
    s3, s2, s1 = _pieces(v_ref)
    a = _nt(s3, x1)
    c = _nt(s2, x2)
    d = _nt(s1, x3)
    part = ((a[2 * k:] + c[k:] + d) + (a[k:2 * k] + c[:k])) + a[:k]

    @pl.when(j == 0)
    def _():
        y_ref[...] = part

    @pl.when(j > 0)
    def _():
        y_ref[...] += part

    if col:
        (c_ref,) = col
        i = pl.program_id(0)
        tw = x_ref.shape[1]
        s = jnp.sum(x, axis=0, keepdims=True)
        sl = pl.ds(pl.multiple_of(j * tw, tw), tw)

        @pl.when(i == 0)
        def _():
            c_ref[:, sl] = s

        @pl.when(i > 0)
        def _():
            c_ref[:, sl] += s


def backward_kernel(x_ref, m_ref, v_ref, o_ref, *col):
    i = pl.program_id(1)
    k = v_ref.shape[0]
    x = _masked(x_ref, m_ref)
    x1, x2, x3 = split(x)
    p = split(v_ref[...])
    ones = [jnp.ones((8, v_ref.shape[1]), BF)] if col else []
    a = jnp.dot(jnp.concatenate(list(p) + ones, axis=0), x1, preferred_element_type=F32)
    c = jnp.dot(jnp.concatenate(list(p[:2]) + ones, axis=0), x2, preferred_element_type=F32)
    d = jnp.dot(jnp.concatenate(list(p[:1]) + ones, axis=0), x3, preferred_element_type=F32)
    part = ((a[2 * k:3 * k] + c[k:2 * k] + d[:k]) + (a[k:2 * k] + c[:k])) + a[:k]

    @pl.when(i == 0)
    def _():
        o_ref[...] = part

    @pl.when(i > 0)
    def _():
        o_ref[...] += part

    if col:
        (c_ref,) = col
        sums = (d[k:k + 1] + c[2 * k:2 * k + 1]) + a[3 * k:3 * k + 1]

        @pl.when(i == 0)
        def _():
            c_ref[...] = sums

        @pl.when(i > 0)
        def _():
            c_ref[...] += sums


def blocks(rows, width):
    tr = 2 * TILE if rows % (2 * TILE) == 0 else TILE
    tw = min(width, 4096)
    return tr, tw


def forward(expression, mexp, bt, with_colsum):
    rows, width = expression.shape
    k = bt.shape[0]
    tr, tw = blocks(rows, width)
    in_specs = [
        pl.BlockSpec((tr, tw), lambda i, j: (i, j)),
        pl.BlockSpec((tr // TILE, 1, tw), lambda i, j: (i, 0, j)),
        pl.BlockSpec((k, tw), lambda i, j: (0, j)),
    ]
    out_specs = [pl.BlockSpec((k, tr), lambda i, j: (0, i))]
    out_shape = [jax.ShapeDtypeStruct((k, rows), F32)]
    if with_colsum:
        out_specs.append(pl.BlockSpec((1, width), lambda i, j: (0, 0)))
        out_shape.append(jax.ShapeDtypeStruct((1, width), F32))
    return pl.pallas_call(
        forward_kernel,
        grid=(rows // tr, width // tw),
        in_specs=in_specs,
        out_specs=out_specs,
        out_shape=out_shape,
        compiler_params=pltpu.CompilerParams(dimension_semantics=("arbitrary", "arbitrary")),
    )(expression, mexp, bt)


def backward(expression, mexp, yt, with_colsum):
    rows, width = expression.shape
    k = yt.shape[0]
    tr, tw = blocks(rows, width)
    out_specs = [pl.BlockSpec((k, tw), lambda j, i: (0, j))]
    out_shape = [jax.ShapeDtypeStruct((k, width), F32)]
    if with_colsum:
        out_specs.append(pl.BlockSpec((1, tw), lambda j, i: (0, j)))
        out_shape.append(jax.ShapeDtypeStruct((1, width), F32))
    return pl.pallas_call(
        backward_kernel,
        grid=(width // tw, rows // tr),
        in_specs=[
            pl.BlockSpec((tr, tw), lambda j, i: (i, j)),
            pl.BlockSpec((tr // TILE, 1, tw), lambda j, i: (i, 0, j)),
            pl.BlockSpec((k, tr), lambda j, i: (0, i)),
        ],
        out_specs=out_specs,
        out_shape=out_shape,
        compiler_params=pltpu.CompilerParams(dimension_semantics=("arbitrary", "arbitrary")),
    )(expression, mexp, yt)


HI = lax.Precision.HIGHEST


def row_gram(a, b):
    return lax.dot_general(a, b, (((1,), (1,)), ((), ())), precision=HI, preferred_element_type=F32)


def left_solve(lower, x):
    return lax.linalg.triangular_solve(lower, x, left_side=True, lower=True)


def right_solve(lower, x):
    return lax.linalg.triangular_solve(lower, x, left_side=False, lower=True, transpose_a=True)


def per_device(expression, tile_mask, start):
    cell_count = lax.axis_size("cell")
    gene_count = lax.axis_size("gene")
    rows, width = expression.shape
    cells = rows * cell_count
    mexp = jnp.repeat(tile_mask.astype(F32), TILE, axis=1)[:, None, :]
    start_t = jnp.transpose(start)

    y_start = forward(expression, mexp, start_t, False)[0]
    start_t = lax.optimization_barrier((start_t, y_start))[0]
    extra = jnp.concatenate([row_gram(start_t, start_t), jnp.sum(y_start, axis=1)[None, :]], axis=0)
    y_start, extra = gene_sum_with(y_start, extra)
    gram0 = extra[:-1]
    row_total = extra[-1]
    lower0 = jnp.linalg.cholesky(gram0)
    current = left_solve(lower0, start_t)
    y = left_solve(lower0, y_start)

    older = None
    older_side = None
    alpha_list = []
    beta_list = []
    for step in range(STEPS):
        if step > 0:
            y, side = gene_sum_with(forward(expression, mexp, last_resid, False)[0],
                                    jnp.dot(last_resid, means, precision=HI))
            y = left_solve(last_lower, y)
            mean_side = left_solve(last_lower, side[:, None])[:, 0]
        basis = [current] if older is None else [current, older]
        if step == 0:
            part, colsum = backward(expression, mexp, y, True)
            proj_part = jnp.stack([row_gram(v, part) for v in basis])
            ride = jnp.concatenate([proj_part.reshape(-1), colsum[0], row_total])
            raw, ride = cell_image_sum(part, ride)
            proj_cell = ride[:proj_part.size].reshape(proj_part.shape)
            means = ride[proj_part.size:proj_part.size + width] / cells
            mean_side = right_solve(lower0, (ride[proj_part.size + width:] / cells)[None, :])[0]
        else:
            part = backward(expression, mexp, y, False)[0]
            proj_part = jnp.stack([row_gram(v, part) for v in basis])
            raw, proj_cell = cell_image_sum(part, proj_part)
        sides = [mean_side] if older is None else [mean_side, older_side]
        proj_raw = butterfly_sum(proj_cell, "gene")
        image = raw / cells - mean_side[:, None] * means[None, :]
        summed = [proj_raw[t] / cells - sides[t][:, None] * mean_side[None, :] for t in range(len(basis))]
        resid = image - jnp.dot(jnp.transpose(summed[0]), current, precision=HI)
        if older is not None:
            resid = resid - jnp.dot(jnp.transpose(summed[1]), older, precision=HI)
        g = butterfly_sum(row_gram(resid, resid), "gene")
        lower = jnp.linalg.cholesky(g)
        fresh = left_solve(lower, resid)
        alpha_list.append(summed[0])
        beta_list.append(jnp.transpose(lower))
        older = current
        older_side = mean_side
        current = fresh
        last_resid = resid
        last_lower = lower
    next_block = jnp.transpose(current) * math.sqrt(width * gene_count)
    return (jnp.stack(alpha_list), jnp.stack(beta_list), next_block)


def solution(mesh):
    in_specs = (P("cell", "gene"), P("cell", "gene"), P("gene", None))
    out_specs = (P(), P(), P("gene", None))
    return jax.shard_map(
        per_device, mesh=mesh, in_specs=in_specs, out_specs=out_specs, check_vma=False
    )
```

```python
import math

import jax
import jax.numpy as jnp
from jax import lax
from jax.experimental import pallas as pl
from jax.experimental.pallas import tpu as pltpu
from jax.sharding import PartitionSpec as P

TILE = 256
STEPS = 2
BF = jnp.bfloat16
F32 = jnp.float32


def split(x):
    p1 = x.astype(BF)
    r1 = x - p1.astype(F32)
    p2 = r1.astype(BF)
    p3 = (r1 - p2.astype(F32)).astype(BF)
    return p1, p2, p3


def butterfly_sum(x, axis):
    n = lax.axis_size(axis)
    if n & (n - 1):
        return lax.psum(x, axis)
    s = 1
    while s < n:
        x = x + lax.ppermute(x, axis, [(i, i ^ s) for i in range(n)])
        s *= 2
    return x


def halving_sum(x, axis, dim):
    n = lax.axis_size(axis)
    if n & (n - 1) or x.shape[dim] % n:
        return lax.psum(x, axis)
    me = lax.axis_index(axis)
    levels = max(n.bit_length() - 2, 0)
    s = 1
    bits = []
    for _ in range(levels):
        half = x.shape[dim] // 2
        bit = (me // s) % 2
        keep = lax.dynamic_slice_in_dim(x, bit * half, half, axis=dim)
        send = lax.dynamic_slice_in_dim(x, (1 - bit) * half, half, axis=dim)
        x = keep + lax.ppermute(send, axis, [(i, i ^ s) for i in range(n)])
        bits.append((s, bit))
        s *= 2
    while s < n:
        x = x + lax.ppermute(x, axis, [(i, i ^ s) for i in range(n)])
        s *= 2
    for s, bit in reversed(bits):
        other = lax.ppermute(x, axis, [(i, i ^ s) for i in range(n)])
        lo_first = jnp.concatenate([x, other], axis=dim)
        hi_first = jnp.concatenate([other, x], axis=dim)
        x = jnp.where(bit == 0, lo_first, hi_first)
    return x


def pack_rows(x, extra):
    w = x.shape[1]
    flat = extra.reshape(-1)
    rows = -(-flat.shape[0] // w)
    flat = jnp.pad(flat, (0, rows * w - flat.shape[0]))
    return jnp.concatenate([x, flat.reshape(rows, w)], axis=0)


def unpack_rows(x, r, extra_shape):
    size = math.prod(extra_shape)
    return x[:r], x[r:].reshape(-1)[:size].reshape(extra_shape)


def gene_sum_with(x, extra):
    r = x.shape[0]
    return unpack_rows(butterfly_sum(pack_rows(x, extra), "gene"), r, extra.shape)


def cell_image_sum(part, extra):
    axis = "cell"
    n = lax.axis_size(axis)
    if n & (n - 1) or part.shape[1] % n:
        return lax.psum(part, axis), lax.psum(extra, axis)
    me = lax.axis_index(axis)
    levels = max(n.bit_length() - 2, 0)
    k = part.shape[0]
    x = part
    s = 1
    bits = []
    for _ in range(levels):
        half = x.shape[1] // 2
        bit = (me // s) % 2
        keep = lax.dynamic_slice_in_dim(x, bit * half, half, axis=1)
        send = lax.dynamic_slice_in_dim(x, (1 - bit) * half, half, axis=1)
        got = lax.ppermute(pack_rows(send, extra), axis, [(i, i ^ s) for i in range(n)])
        got_x, got_e = unpack_rows(got, k, extra.shape)
        x = keep + got_x
        extra = extra + got_e
        bits.append((s, bit))
        s *= 2
    while s < n:
        got = lax.ppermute(pack_rows(x, extra), axis, [(i, i ^ s) for i in range(n)])
        got_x, got_e = unpack_rows(got, k, extra.shape)
        x = x + got_x
        extra = extra + got_e
        s *= 2
    for s, bit in reversed(bits):
        other = lax.ppermute(x, axis, [(i, i ^ s) for i in range(n)])
        lo_first = jnp.concatenate([x, other], axis=1)
        hi_first = jnp.concatenate([other, x], axis=1)
        x = jnp.where(bit == 0, lo_first, hi_first)
    return x, extra


def _nt(a, b):
    return lax.dot_general(a, b, (((1,), (1,)), ((), ())), preferred_element_type=F32)


def _masked(x_ref, m_ref):
    tr, tw = x_ref.shape
    x = x_ref[...].reshape(tr // TILE, TILE, tw) * m_ref[...]
    return x.reshape(tr, tw)


def _pieces(v_ref):
    p = split(v_ref[...])
    return jnp.concatenate(p, axis=0), jnp.concatenate(p[:2], axis=0), p[0]


def forward_kernel(x_ref, m_ref, v_ref, y_ref, *col):
    j = pl.program_id(1)
    k = v_ref.shape[0]
    x = _masked(x_ref, m_ref)
    x1, x2, x3 = split(x)
    s3, s2, s1 = _pieces(v_ref)
    a = _nt(s3, x1)
    c = _nt(s2, x2)
    d = _nt(s1, x3)
    part = ((a[2 * k:] + c[k:] + d) + (a[k:2 * k] + c[:k])) + a[:k]

    @pl.when(j == 0)
    def _():
        y_ref[...] = part

    @pl.when(j > 0)
    def _():
        y_ref[...] += part

    if col:
        (c_ref,) = col
        i = pl.program_id(0)
        tw = x_ref.shape[1]
        s = jnp.sum(x, axis=0, keepdims=True)
        sl = pl.ds(pl.multiple_of(j * tw, tw), tw)

        @pl.when(i == 0)
        def _():
            c_ref[:, sl] = s

        @pl.when(i > 0)
        def _():
            c_ref[:, sl] += s


def backward_kernel(x_ref, m_ref, v_ref, o_ref, *col):
    i = pl.program_id(1)
    k = v_ref.shape[0]
    x = _masked(x_ref, m_ref)
    x1, x2, x3 = split(x)
    p = split(v_ref[...])
    ones = [jnp.ones((8, v_ref.shape[1]), BF)] if col else []
    a = jnp.dot(jnp.concatenate(list(p) + ones, axis=0), x1, preferred_element_type=F32)
    c = jnp.dot(jnp.concatenate(list(p[:2]) + ones, axis=0), x2, preferred_element_type=F32)
    d = jnp.dot(jnp.concatenate(list(p[:1]) + ones, axis=0), x3, preferred_element_type=F32)
    part = ((a[2 * k:3 * k] + c[k:2 * k] + d[:k]) + (a[k:2 * k] + c[:k])) + a[:k]

    @pl.when(i == 0)
    def _():
        o_ref[...] = part

    @pl.when(i > 0)
    def _():
        o_ref[...] += part

    if col:
        (c_ref,) = col
        sums = (d[k:k + 1] + c[2 * k:2 * k + 1]) + a[3 * k:3 * k + 1]

        @pl.when(i == 0)
        def _():
            c_ref[...] = sums

        @pl.when(i > 0)
        def _():
            c_ref[...] += sums


def blocks(rows, width):
    tr = 2 * TILE if rows % (2 * TILE) == 0 else TILE
    tw = min(width, 4096)
    return tr, tw


def forward(expression, mexp, bt, with_colsum):
    rows, width = expression.shape
    k = bt.shape[0]
    tr, tw = blocks(rows, width)
    in_specs = [
        pl.BlockSpec((tr, tw), lambda i, j: (i, j)),
        pl.BlockSpec((tr // TILE, 1, tw), lambda i, j: (i, 0, j)),
        pl.BlockSpec((k, tw), lambda i, j: (0, j)),
    ]
    out_specs = [pl.BlockSpec((k, tr), lambda i, j: (0, i))]
    out_shape = [jax.ShapeDtypeStruct((k, rows), F32)]
    if with_colsum:
        out_specs.append(pl.BlockSpec((1, width), lambda i, j: (0, 0)))
        out_shape.append(jax.ShapeDtypeStruct((1, width), F32))
    return pl.pallas_call(
        forward_kernel,
        grid=(rows // tr, width // tw),
        in_specs=in_specs,
        out_specs=out_specs,
        out_shape=out_shape,
        compiler_params=pltpu.CompilerParams(dimension_semantics=("arbitrary", "arbitrary")),
    )(expression, mexp, bt)


def backward(expression, mexp, yt, with_colsum):
    rows, width = expression.shape
    k = yt.shape[0]
    tr, tw = blocks(rows, width)
    out_specs = [pl.BlockSpec((k, tw), lambda j, i: (0, j))]
    out_shape = [jax.ShapeDtypeStruct((k, width), F32)]
    if with_colsum:
        out_specs.append(pl.BlockSpec((1, tw), lambda j, i: (0, j)))
        out_shape.append(jax.ShapeDtypeStruct((1, width), F32))
    return pl.pallas_call(
        backward_kernel,
        grid=(width // tw, rows // tr),
        in_specs=[
            pl.BlockSpec((tr, tw), lambda j, i: (i, j)),
            pl.BlockSpec((tr // TILE, 1, tw), lambda j, i: (i, 0, j)),
            pl.BlockSpec((k, tr), lambda j, i: (0, i)),
        ],
        out_specs=out_specs,
        out_shape=out_shape,
        compiler_params=pltpu.CompilerParams(dimension_semantics=("arbitrary", "arbitrary")),
    )(expression, mexp, yt)


HI = lax.Precision.HIGHEST


def row_gram(a, b):
    return lax.dot_general(a, b, (((1,), (1,)), ((), ())), precision=HI, preferred_element_type=F32)


def left_solve(lower, x):
    return lax.linalg.triangular_solve(lower, x, left_side=True, lower=True)


def right_solve(lower, x):
    return lax.linalg.triangular_solve(lower, x, left_side=False, lower=True, transpose_a=True)


def per_device(expression, tile_mask, start):
    cell_count = lax.axis_size("cell")
    gene_count = lax.axis_size("gene")
    rows, width = expression.shape
    cells = rows * cell_count
    mexp = jnp.repeat(tile_mask.astype(F32), TILE, axis=1)[:, None, :]
    start_t = jnp.transpose(start)

    y_start = forward(expression, mexp, start_t, False)[0]
    start_t = lax.optimization_barrier((start_t, y_start))[0]
    extra = jnp.concatenate([row_gram(start_t, start_t), jnp.sum(y_start, axis=1)[None, :]], axis=0)
    y_start, extra = gene_sum_with(y_start, extra)
    gram0 = extra[:-1]
    row_total = extra[-1]
    lower0 = jnp.linalg.cholesky(gram0)
    current = left_solve(lower0, start_t)
    y = y_start

    older = None
    older_side = None
    alpha_list = []
    beta_list = []
    for step in range(STEPS):
        if step > 0:
            y, side = gene_sum_with(forward(expression, mexp, last_resid, False)[0],
                                    jnp.dot(last_resid, means, precision=HI))
            y = left_solve(last_lower, y)
            mean_side = left_solve(last_lower, side[:, None])[:, 0]
        basis = [current] if older is None else [current, older]
        if step == 0:
            part, colsum = backward(expression, mexp, y, True)
            proj_part = jnp.stack([row_gram(v, part) for v in basis])
            ride = jnp.concatenate([proj_part.reshape(-1), colsum[0], row_total])
            raw, ride = cell_image_sum(part, ride)
            raw = left_solve(lower0, raw)
            proj_cell = right_solve(lower0, ride[:proj_part.size].reshape(proj_part.shape)[0])[None]
            means = ride[proj_part.size:proj_part.size + width] / cells
            mean_side = right_solve(lower0, (ride[proj_part.size + width:] / cells)[None, :])[0]
        else:
            part = backward(expression, mexp, y, False)[0]
            proj_part = jnp.stack([row_gram(v, part) for v in basis])
            raw, proj_cell = cell_image_sum(part, proj_part)
        sides = [mean_side] if older is None else [mean_side, older_side]
        proj_raw = butterfly_sum(proj_cell, "gene")
        image = raw / cells - mean_side[:, None] * means[None, :]
        summed = [proj_raw[t] / cells - sides[t][:, None] * mean_side[None, :] for t in range(len(basis))]
        resid = image - jnp.dot(jnp.transpose(summed[0]), current, precision=HI)
        if older is not None:
            resid = resid - jnp.dot(jnp.transpose(summed[1]), older, precision=HI)
        g = butterfly_sum(row_gram(resid, resid), "gene")
        lower = jnp.linalg.cholesky(g)
        fresh = left_solve(lower, resid)
        alpha_list.append(summed[0])
        beta_list.append(jnp.transpose(lower))
        older = current
        older_side = mean_side
        current = fresh
        last_resid = resid
        last_lower = lower
    next_block = jnp.transpose(current) * math.sqrt(width * gene_count)
    return (jnp.stack(alpha_list), jnp.stack(beta_list), next_block)


def solution(mesh):
    in_specs = (P("cell", "gene"), P("cell", "gene"), P("gene", None))
    out_specs = (P(), P(), P("gene", None))
    return jax.shard_map(
        per_device, mesh=mesh, in_specs=in_specs, out_specs=out_specs, check_vma=False
    )
```
